32 devices in a mesh: sec: 4 (over y, x), tile: 8 (over z, core).
Axes of the slice: x: 2, y: 2, z: 4, core: 2. Of those that a mesh axis runs over, the one named last changes fastest.
Arguments:
- tracers: bfloat16 [4, 72, 32, 1024], P(None, None, 'sec', 'tile'), may hold values from -6 to 6
- courant: bfloat16 [2, 72, 32, 1024], P(None, None, 'sec', 'tile'), may hold values from -0.44921875 to 0.44921875
- destination: int32 [32, 8], P(('sec', 'tile')), may hold values from 0 to 7, each once within a row
- diffusion: bfloat16 [32, 72, 72], P(('sec', 'tile')), may hold values from 0 to 1.25
- band: int32 [32], P(('sec', 'tile')), may hold values from 0 to 15
- band_table: bfloat16 [16, 72, 72], replicated, may hold values from -0.75 to 0.75
Outputs:
- column_state: bfloat16 [4, 72, 256, 128], P(None, None, ('sec', 'tile'))
The draws below stay inside these ranges and needn't reach their ends.
Inputs may be any that keep to these rules, and one draw needn't show every extreme that they name: Each row of destination names every column block of its group once.
All inputs are finite; a program needn't handle non-finite values.
Results may differ from the reference program's by a relative error of at most 0.0066.
Values may be sent and summed in bfloat16 or wider, within the bound.
No kernel may reach another device: no remote copies, remote signals or barrier semaphores. Data moves between devices by JAX's collectives and lax.ppermute only.
A program may use at most 128 MiB of HBM per device.

```python
import jax
import jax.numpy as jnp
from jax import lax

TR = 4
LEV = 72
NBANDS = 16
STEPS = 3
HY = 128
HX = 8
NX = 32
NY = 1024
NBLK = 32
NROWS = 256
N_SEC = 4
N_TILE = 8


def draw_diffusion(key, part):
    first, second = jax.random.split(key)
    levels = jnp.arange(LEV, dtype=jnp.int32)
    distance = jnp.abs(levels[:, None] - levels[None, :])
    falloff = jnp.power(jnp.float32(0.5), distance.astype(jnp.float32))
    spread = jax.random.uniform(first, (NBLK, LEV, LEV), jnp.float32, 0.3, 1.0)
    centre = jax.random.uniform(second, (NBLK, LEV, LEV), jnp.float32, 0.9, 1.2)
    matrix = jnp.where(distance[None] == 0, centre, 0.4 * falloff[None] * spread)
    return matrix.astype(jnp.bfloat16)


def set_ends(values, stream_key, smallest, high):
    longest = values.shape.index(max(values.shape))
    spots = []
    for shift in (0, 1):
        where = [jax.random.randint(jax.random.fold_in(stream_key, axis), (), 0, length) for axis, length in enumerate(values.shape)]
        where[longest] = (where[longest] + shift) % values.shape[longest]
        spots.append(tuple(where))
    return values.at[spots[0]].set(smallest).at[spots[1]].set(high)


def shard_levels(key, dims, cuts, least, top_value):
    def one(dim, parts):
        draws = jax.random.uniform(jax.random.fold_in(jax.random.fold_in(key, 6), dim), (parts,), jnp.float32, least / len(cuts), top_value / len(cuts))
        return jnp.repeat(jnp.exp(draws), dims[dim] // parts).reshape((-1,) + (1,) * (len(dims) - dim - 1))

    level = one(*cuts[0])
    for cut in cuts[1:]:
        level = level * one(*cut)
    return level


def centred(rng, extent, scale, reach, cuts=(), kind=jnp.bfloat16):
    loudness = shard_levels(rng, extent, cuts, -0.22, 0.18) if cuts else 1.0
    array = jax.random.normal(rng, extent, jnp.float32) * scale * loudness
    return jnp.minimum(jnp.maximum(array, -reach), reach).astype(kind)


def setup_inputs(seed: int = 0) -> dict:
    seeds = jax.random.split(jax.random.key(seed), 7)
    return {
        "tracers": centred(seeds[0], (TR, LEV, NX, NY), 1.0, 6.0, ((2, 4), (3, 8))),
        "courant": jnp.clip(jax.random.uniform(seeds[1], (2, LEV, NX, NY), jnp.float32, -0.44921875, 0.44921875) * shard_levels(seeds[1], (2, LEV, NX, NY), ((2, 4), (3, 8)), -0.4, 0.0), -0.44921875, 0.44921875).astype(jnp.bfloat16),
        "destination": jax.vmap(lambda own: jax.random.permutation(own, N_TILE))(jax.random.split(seeds[2], NBLK)).reshape((NBLK, N_TILE)).astype(jnp.int32),
        "diffusion": draw_diffusion(jax.random.fold_in(seeds[6], 71), 0),
        "band": set_ends(jax.random.randint(seeds[4], (NBLK,), 0, NBANDS), jax.random.fold_in(seeds[4], 1), 0, NBANDS - 1).astype(jnp.int32),
        "band_table": centred(seeds[5], (NBANDS, LEV, LEV), LEV ** -0.5, 0.75),
    }


def advect_one(pair):
    field, cour = pair
    q = field.astype(jnp.float32)
    cx = cour[0].astype(jnp.float32)
    cy = cour[1].astype(jnp.float32)
    north = jnp.roll(q, -1, 1)
    south = jnp.roll(q, 1, 1)
    east = jnp.roll(q, -1, 2)
    west = jnp.roll(q, 1, 2)
    out = q - 0.5 * cx * (north - south) + 0.5 * cx * cx * (north - 2.0 * q + south)
    out = out - 0.5 * cy * (east - west) + 0.5 * cy * cy * (east - 2.0 * q + west)
    return out.astype(jnp.bfloat16)


def reference(tracers, courant, destination, diffusion, band, band_table):
    adv = tracers
    for step in range(STEPS):
        adv = lax.map(lambda field: advect_one((field, courant)), adv)
    order = jnp.argsort(destination, axis=1).astype(jnp.int32)
    shaped = adv.reshape(TR, LEV, N_SEC, HX, N_TILE, HY).transpose(2, 4, 3, 0, 1, 5)
    sources = jnp.arange(N_TILE, dtype=jnp.int32)

    def block(index):
        sec_index = index // N_TILE
        col_index = index % N_TILE
        order_group = lax.dynamic_slice_in_dim(order, (sec_index * N_TILE).astype(jnp.int32), N_TILE, 0)
        rows_used = jnp.take(order_group, col_index, axis=1)
        group = lax.dynamic_index_in_dim(shaped, sec_index, 0, keepdims=False)
        piece = group[sources, rows_used]
        state = piece.transpose(1, 2, 0, 3).astype(jnp.float32)
        inverse = diffusion[index].astype(jnp.float32)
        diffused = jnp.einsum('kl,tliy->tkiy', inverse, state, precision=lax.Precision.HIGHEST)
        diffused16 = diffused.astype(jnp.bfloat16).astype(jnp.float32)
        radiation = band_table[band[index]].astype(jnp.float32)
        heating = jnp.einsum('kl,tliy->tkiy', radiation, diffused16, precision=lax.Precision.HIGHEST)
        return (diffused + heating).astype(jnp.bfloat16)

    blocks = lax.map(block, jnp.arange(NBLK, dtype=jnp.int32))
    return blocks.transpose(1, 2, 0, 3, 4).reshape(TR, LEV, NROWS, HY)
```

```python
import jax
import jax.numpy as jnp
from jax import lax
from jax.sharding import PartitionSpec as P

STEPS = 3


def with_halo(cells, sides, width):
    for axis, dim in sides:
        count = lax.axis_size(axis)
        head = lax.slice_in_dim(cells, 0, width, axis=dim)
        tail = lax.slice_in_dim(cells, cells.shape[dim] - width, cells.shape[dim], axis=dim)
        cells = jnp.concatenate(
            [
                lax.ppermute(tail, axis, [(i, (i + 1) % count) for i in range(count)]),
                cells,
                lax.ppermute(head, axis, [((i + 1) % count, i) for i in range(count)]),
            ],
            axis=dim,
        )
    return cells


def advect_tile(padded, courant):
    centre = padded[:, :, 1:-1, 1:-1].astype(jnp.float32)
    north = padded[:, :, 2:, 1:-1].astype(jnp.float32)
    south = padded[:, :, :-2, 1:-1].astype(jnp.float32)
    east = padded[:, :, 1:-1, 2:].astype(jnp.float32)
    west = padded[:, :, 1:-1, :-2].astype(jnp.float32)
    cx = courant[0].astype(jnp.float32)
    cy = courant[1].astype(jnp.float32)
    out = centre - 0.5 * cx * (north - south) + 0.5 * cx * cx * (north - 2.0 * centre + south)
    out = out - 0.5 * cy * (east - west) + 0.5 * cy * cy * (east - 2.0 * centre + west)
    return out.astype(jnp.bfloat16)


def per_device(tracers, courant, destination, diffusion, band, band_table):
    count = tracers.shape[0]
    fields = jnp.concatenate([tracers, courant], axis=0)
    padded = with_halo(fields, (("sec", 2), ("tile", 3)), STEPS)
    advected = padded[:count]
    wind = padded[count:]
    for step in range(STEPS):
        wind = wind[:, :, 1:-1, 1:-1]
        advected = advect_tile(advected, wind)
    order = jnp.argsort(destination[0])
    band_count = band_table.shape[0]
    ordered = jnp.take(advected, order, axis=2)
    received = lax.all_to_all(ordered, "tile", split_axis=2, concat_axis=2, tiled=True)
    inverse = diffusion[0]
    diffused = jnp.einsum("kl,tlxy->tkxy", inverse, received, preferred_element_type=jnp.float32)
    diffused16 = diffused.astype(jnp.bfloat16)
    picked = (jnp.arange(band_count, dtype=jnp.int32) == band[0])[:, None, None]
    radiation = jnp.sum(jnp.where(picked, band_table, jnp.zeros_like(band_table)), axis=0)
    heating = jnp.einsum("kl,tlxy->tkxy", radiation, diffused16, preferred_element_type=jnp.float32)
    return (diffused + heating).astype(jnp.bfloat16)


def solution(mesh):
    placed = (
        P(None, None, "sec", "tile"),
        P(None, None, "sec", "tile"),
        P(("sec", "tile"), None),
        P(("sec", "tile"), None, None),
        P(("sec", "tile")),
        P(),
    )
    return jax.shard_map(
        per_device,
        mesh=mesh,
        in_specs=placed,
        out_specs=P(None, None, ("sec", "tile"), None),
        check_vma=False,
    )
```

```python
import jax
import jax.numpy as jnp
from jax import lax
from jax.sharding import PartitionSpec as P

STEPS = 3


def with_halo(cells, sides, width):
    for axis, dim in sides:
        count = lax.axis_size(axis)
        head = lax.slice_in_dim(cells, 0, width, axis=dim)
        tail = lax.slice_in_dim(cells, cells.shape[dim] - width, cells.shape[dim], axis=dim)
        cells = jnp.concatenate(
            [
                lax.ppermute(tail, axis, [(i, (i + 1) % count) for i in range(count)]),
                cells,
                lax.ppermute(head, axis, [((i + 1) % count, i) for i in range(count)]),
            ],
            axis=dim,
        )
    return cells


def advect_tile(padded, courant):
    centre = padded[:, :, 1:-1, 1:-1].astype(jnp.float32)
    north = padded[:, :, 2:, 1:-1].astype(jnp.float32)
    south = padded[:, :, :-2, 1:-1].astype(jnp.float32)
    east = padded[:, :, 1:-1, 2:].astype(jnp.float32)
    west = padded[:, :, 1:-1, :-2].astype(jnp.float32)
    cx = courant[0].astype(jnp.float32)
    cy = courant[1].astype(jnp.float32)
    out = centre - 0.5 * cx * (north - south) + 0.5 * cx * cx * (north - 2.0 * centre + south)
    out = out - 0.5 * cy * (east - west) + 0.5 * cy * cy * (east - 2.0 * centre + west)
    return out.astype(jnp.bfloat16)


CHUNKS = 2


def advect_levels(tracers, courant):
    count = tracers.shape[0]
    fields = jnp.concatenate([tracers, courant], axis=0)
    padded = with_halo(fields, (("sec", 2), ("tile", 3)), STEPS)
    advected = padded[:count]
    wind = padded[count:]
    for step in range(STEPS):
        wind = wind[:, :, 1:-1, 1:-1]
        advected = advect_tile(advected, wind)
    return advected


def regroup(advected, order):
    count = lax.axis_size("tile")
    if count > 8:
        ordered = jnp.take(advected, order, axis=2)
        return lax.all_to_all(ordered, "tile", split_axis=2, concat_axis=2, tiled=True)
    me = lax.axis_index("tile")
    pieces = []
    for shift in range(count):
        row = jnp.take(order, (me + shift) % count)
        piece = lax.dynamic_slice_in_dim(advected, row, 1, axis=2)
        if shift:
            piece = lax.ppermute(piece, "tile", [(i, (i + shift) % count) for i in range(count)])
        pieces.append(piece)
    stacked = jnp.concatenate(pieces, axis=2)
    source = (me - jnp.arange(count, dtype=jnp.int32)) % count
    return jnp.take(stacked, source, axis=2)


def per_device(tracers, courant, destination, diffusion, band, band_table):
    order = jnp.argsort(destination[0]).astype(jnp.int32)
    levels = tracers.shape[1]
    size = -(-levels // CHUNKS)
    pieces = []
    for start in range(0, levels, size):
        stop = min(start + size, levels)
        advected = advect_levels(tracers[:, start:stop], courant[:, start:stop])
        pieces.append(regroup(advected, order))
    received = jnp.concatenate(pieces, axis=1)
    band_count = band_table.shape[0]
    inverse = diffusion[0]
    diffused = jnp.einsum("kl,tlxy->tkxy", inverse, received, preferred_element_type=jnp.float32)
    diffused16 = diffused.astype(jnp.bfloat16)
    picked = (jnp.arange(band_count, dtype=jnp.int32) == band[0])[:, None, None]
    radiation = jnp.sum(jnp.where(picked, band_table, jnp.zeros_like(band_table)), axis=0)
    heating = jnp.einsum("kl,tlxy->tkxy", radiation, diffused16, preferred_element_type=jnp.float32)
    return (diffused + heating).astype(jnp.bfloat16)


def solution(mesh):
    placed = (
        P(None, None, "sec", "tile"),
        P(None, None, "sec", "tile"),
        P(("sec", "tile"), None),
        P(("sec", "tile"), None, None),
        P(("sec", "tile")),
        P(),
    )
    return jax.shard_map(
        per_device,
        mesh=mesh,
        in_specs=placed,
        out_specs=P(None, None, ("sec", "tile"), None),
        check_vma=False,
    )
```

```python
import functools

import jax
import jax.numpy as jnp
from jax import lax
from jax.experimental import pallas as pl
from jax.experimental.pallas import tpu as pltpu
from jax.sharding import PartitionSpec as P

STEPS = 3


def stencil_kernel(step, emit, *refs):
    if step:
        q_ref, wind_ref, north_ref, south_ref, east_ref, west_ref = refs[:6]
        refs = refs[6:]
    else:
        q_ref = refs[0]
        refs = refs[1:]
    if step:
        out_ref = refs[0]
        refs = refs[1:]
    if emit:
        top_ref, bottom_ref, first_ref, last_ref = refs[:4]
        refs = refs[4:]
    new_scr, row_scr = refs

    count, levels, rows, cols = q_ref.shape
    planes = levels * rows

    if step:
        cx = wind_ref[0].astype(jnp.float32)
        cy = wind_ref[1].astype(jnp.float32)
        half_x = 0.5 * cx
        full_x = half_x * cx
        half_y = 0.5 * cy
        full_y = half_y * cy
        strips = jnp.zeros((cols, count * planes), jnp.float32)
        strips = jnp.where(
            lax.broadcasted_iota(jnp.int32, strips.shape, 0) == 0,
            east_ref[...].astype(jnp.float32),
            jnp.where(
                lax.broadcasted_iota(jnp.int32, strips.shape, 0) == 1,
                west_ref[...].astype(jnp.float32),
                strips,
            ),
        )
        columns = strips.T
        sub = lax.broadcasted_iota(jnp.int32, (levels, rows, cols), 1)
        lane = lax.broadcasted_iota(jnp.int32, (levels, rows, cols), 2)

    for field in range(count):
        centre = q_ref[field].astype(jnp.float32)
        if step:
            row_scr[:, rows - 1, :] = north_ref[field].astype(jnp.float32)
            north_halo = row_scr[...]
            row_scr[:, 0, :] = south_ref[field].astype(jnp.float32)
            south_halo = row_scr[...]
            north = jnp.where(sub == rows - 1, north_halo, pltpu.roll(centre, rows - 1, 1))
            south = jnp.where(sub == 0, south_halo, pltpu.roll(centre, 1, 1))
            side = columns[field * planes:(field + 1) * planes].reshape(levels, rows, cols)
            side = pltpu.roll(side, cols - 1, 2)
            east = jnp.where(lane == cols - 1, side, pltpu.roll(centre, cols - 1, 2))
            west = jnp.where(lane == 0, side, pltpu.roll(centre, 1, 2))
            out = centre - half_x * (north - south) + full_x * (north - 2.0 * centre + south)
            out = out - half_y * (east - west) + full_y * (east - 2.0 * centre + west)
            new = out.astype(jnp.bfloat16)
            out_ref[field] = new
        else:
            new = q_ref[field]
        if emit:
            new_scr[...] = new.astype(jnp.float32)
            top_ref[field] = new_scr[:, 0, :].astype(top_ref.dtype)
            bottom_ref[field] = new_scr[:, rows - 1, :].astype(bottom_ref.dtype)
            flat = new.astype(jnp.float32).reshape(planes, cols).astype(jnp.bfloat16)
            pick = lax.broadcasted_iota(jnp.int32, (8, cols), 1)
            which = lax.broadcasted_iota(jnp.int32, (8, cols), 0)
            onehot = jnp.where(
                ((which == 0) & (pick == 0)) | ((which == 1) & (pick == cols - 1)), 1.0, 0.0
            ).astype(jnp.bfloat16)
            edges = lax.dot_general(
                onehot, flat, (((1,), (1,)), ((), ())), preferred_element_type=jnp.float32
            )
            first_ref[:, field * planes:(field + 1) * planes] = edges[0:1].astype(first_ref.dtype)
            last_ref[:, field * planes:(field + 1) * planes] = edges[1:2].astype(last_ref.dtype)


def stencil_call(step, emit, q, *extra):
    count, levels, rows, cols = q.shape
    planes = levels * rows
    outs = []
    if step:
        outs.append(jax.ShapeDtypeStruct(q.shape, q.dtype))
    if emit:
        outs += [
            jax.ShapeDtypeStruct((count, levels, cols), q.dtype),
            jax.ShapeDtypeStruct((count, levels, cols), q.dtype),
            jax.ShapeDtypeStruct((1, count * planes), q.dtype),
            jax.ShapeDtypeStruct((1, count * planes), q.dtype),
        ]
    vmem = pl.BlockSpec(memory_space=pltpu.VMEM)
    return pl.pallas_call(
        functools.partial(stencil_kernel, step, emit),
        out_shape=tuple(outs),
        in_specs=[vmem] * (1 + len(extra)),
        out_specs=tuple([vmem] * len(outs)),
        scratch_shapes=[
            pltpu.VMEM((levels, rows, cols), jnp.float32),
            pltpu.VMEM((levels, rows, cols), jnp.float32),
        ],
    )(q, *extra)


def exchange(top, bottom, first, last):
    sec = lax.axis_size("sec")
    tile = lax.axis_size("tile")
    north = lax.ppermute(top, "sec", [(i, (i - 1) % sec) for i in range(sec)])
    south = lax.ppermute(bottom, "sec", [(i, (i + 1) % sec) for i in range(sec)])
    east = lax.ppermute(first, "tile", [(i, (i - 1) % tile) for i in range(tile)])
    west = lax.ppermute(last, "tile", [(i, (i + 1) % tile) for i in range(tile)])
    return north, south, east, west


def per_device(tracers, courant, destination, diffusion, band, band_table):
    halos = stencil_call(0, True, tracers)
    advected = tracers
    for step in range(STEPS):
        emit = step < STEPS - 1
        result = stencil_call(1, emit, advected, courant, *exchange(*halos))
        advected = result[0]
        halos = result[1:]
    order = jnp.argsort(destination[0])
    band_count = band_table.shape[0]
    ordered = jnp.take(advected, order, axis=2)
    received = lax.all_to_all(ordered, "tile", split_axis=2, concat_axis=2, tiled=True)
    inverse = diffusion[0]
    diffused = jnp.einsum("kl,tlxy->tkxy", inverse, received, preferred_element_type=jnp.float32)
    diffused16 = diffused.astype(jnp.bfloat16)
    picked = (jnp.arange(band_count, dtype=jnp.int32) == band[0])[:, None, None]
    radiation = jnp.sum(jnp.where(picked, band_table, jnp.zeros_like(band_table)), axis=0)
    heating = jnp.einsum("kl,tlxy->tkxy", radiation, diffused16, preferred_element_type=jnp.float32)
    return (diffused + heating).astype(jnp.bfloat16)


def solution(mesh):
    placed = (
        P(None, None, "sec", "tile"),
        P(None, None, "sec", "tile"),
        P(("sec", "tile"), None),
        P(("sec", "tile"), None, None),
        P(("sec", "tile")),
        P(),
    )
    return jax.shard_map(
        per_device,
        mesh=mesh,
        in_specs=placed,
        out_specs=P(None, None, ("sec", "tile"), None),
        check_vma=False,
    )
```

```python
import functools

import jax
import jax.numpy as jnp
from jax import lax
from jax.experimental import pallas as pl
from jax.experimental.pallas import tpu as pltpu
from jax.sharding import PartitionSpec as P

STEPS = 3


def stencil_kernel(step, emit, last, *refs):
    if last:
        order_ref = refs[0]
        refs = refs[1:]
    if step:
        q_ref, wind_ref, north_ref, south_ref, east_ref, west_ref = refs[:6]
        refs = refs[6:]
    else:
        q_ref = refs[0]
        refs = refs[1:]
    if step:
        out_ref = refs[0]
        refs = refs[1:]
    if emit:
        top_ref, bottom_ref, first_ref, last_ref = refs[:4]
        refs = refs[4:]
    new_scr, row_scr = refs

    count, levels, rows, cols = q_ref.shape
    planes = levels * rows

    if step:
        cx = wind_ref[0].astype(jnp.float32)
        cy = wind_ref[1].astype(jnp.float32)
        half_x = 0.5 * cx
        full_x = half_x * cx
        half_y = 0.5 * cy
        full_y = half_y * cy
        strips = jnp.zeros((cols, count * planes), jnp.float32)
        strips = jnp.where(
            lax.broadcasted_iota(jnp.int32, strips.shape, 0) == 0,
            east_ref[...].astype(jnp.float32),
            jnp.where(
                lax.broadcasted_iota(jnp.int32, strips.shape, 0) == 1,
                west_ref[...].astype(jnp.float32),
                strips,
            ),
        )
        columns = strips.T
        sub = lax.broadcasted_iota(jnp.int32, (levels, rows, cols), 1)
        lane = lax.broadcasted_iota(jnp.int32, (levels, rows, cols), 2)

    for field in range(count):
        centre = q_ref[field].astype(jnp.float32)
        if step:
            row_scr[:, rows - 1, :] = north_ref[field].astype(jnp.float32)
            north_halo = row_scr[...]
            row_scr[:, 0, :] = south_ref[field].astype(jnp.float32)
            south_halo = row_scr[...]
            north = jnp.where(sub == rows - 1, north_halo, pltpu.roll(centre, rows - 1, 1))
            south = jnp.where(sub == 0, south_halo, pltpu.roll(centre, 1, 1))
            side = columns[field * planes:(field + 1) * planes].reshape(levels, rows, cols)
            side = pltpu.roll(side, cols - 1, 2)
            east = jnp.where(lane == cols - 1, side, pltpu.roll(centre, cols - 1, 2))
            west = jnp.where(lane == 0, side, pltpu.roll(centre, 1, 2))
            out = centre - half_x * (north - south) + full_x * (north - 2.0 * centre + south)
            out = out - half_y * (east - west) + full_y * (east - 2.0 * centre + west)
            new = out.astype(jnp.bfloat16)
            if last:
                new_scr[...] = new.astype(jnp.float32)
                picked = [new_scr[:, row, :] for row in range(rows)]
                for slot in range(rows):
                    wanted = order_ref[slot]
                    value = picked[0]
                    for row in range(1, rows):
                        value = jnp.where(wanted == row, picked[row], value)
                    out_ref[slot, field] = value.astype(out_ref.dtype)
            else:
                out_ref[field] = new
        else:
            new = q_ref[field]
        if emit:
            new_scr[...] = new.astype(jnp.float32)
            top_ref[field] = new_scr[:, 0, :].astype(top_ref.dtype)
            bottom_ref[field] = new_scr[:, rows - 1, :].astype(bottom_ref.dtype)
            flat = new.astype(jnp.float32).reshape(planes, cols).astype(jnp.bfloat16)
            pick = lax.broadcasted_iota(jnp.int32, (8, cols), 1)
            which = lax.broadcasted_iota(jnp.int32, (8, cols), 0)
            onehot = jnp.where(
                ((which == 0) & (pick == 0)) | ((which == 1) & (pick == cols - 1)), 1.0, 0.0
            ).astype(jnp.bfloat16)
            edges = lax.dot_general(
                onehot, flat, (((1,), (1,)), ((), ())), preferred_element_type=jnp.float32
            )
            first_ref[:, field * planes:(field + 1) * planes] = edges[0:1].astype(first_ref.dtype)
            last_ref[:, field * planes:(field + 1) * planes] = edges[1:2].astype(last_ref.dtype)


def stencil_call(step, emit, q, *extra, order=None):
    count, levels, rows, cols = q.shape
    planes = levels * rows
    last = order is not None
    outs = []
    if last:
        outs.append(jax.ShapeDtypeStruct((rows, count, levels, cols), q.dtype))
    elif step:
        outs.append(jax.ShapeDtypeStruct(q.shape, q.dtype))
    if emit:
        outs += [
            jax.ShapeDtypeStruct((count, levels, cols), q.dtype),
            jax.ShapeDtypeStruct((count, levels, cols), q.dtype),
            jax.ShapeDtypeStruct((1, count * planes), q.dtype),
            jax.ShapeDtypeStruct((1, count * planes), q.dtype),
        ]
    vmem = pl.BlockSpec(memory_space=pltpu.VMEM)
    ins = [vmem] * (1 + len(extra))
    operands = (q,) + extra
    if last:
        ins = [pl.BlockSpec(memory_space=pltpu.SMEM)] + ins
        operands = (order,) + operands
    return pl.pallas_call(
        functools.partial(stencil_kernel, step, emit, last),
        out_shape=tuple(outs),
        in_specs=ins,
        out_specs=tuple([vmem] * len(outs)),
        scratch_shapes=[
            pltpu.VMEM((levels, rows, cols), jnp.float32),
            pltpu.VMEM((levels, rows, cols), jnp.float32),
        ],
    )(*operands)


def exchange(top, bottom, first, last):
    sec = lax.axis_size("sec")
    tile = lax.axis_size("tile")
    north = lax.ppermute(top, "sec", [(i, (i - 1) % sec) for i in range(sec)])
    south = lax.ppermute(bottom, "sec", [(i, (i + 1) % sec) for i in range(sec)])
    east = lax.ppermute(first, "tile", [(i, (i - 1) % tile) for i in range(tile)])
    west = lax.ppermute(last, "tile", [(i, (i + 1) % tile) for i in range(tile)])
    return north, south, east, west


def per_device(tracers, courant, destination, diffusion, band, band_table):
    order = jnp.argsort(destination[0]).astype(jnp.int32)
    halos = stencil_call(0, True, tracers)
    advected = tracers
    for step in range(STEPS):
        emit = step < STEPS - 1
        final = None if emit or tracers.shape[2] > 8 else order
        result = stencil_call(1, emit, advected, courant, *exchange(*halos), order=final)
        advected = result[0]
        halos = result[1:]
    if tracers.shape[2] > 8:
        advected = jnp.take(advected, order, axis=2).transpose(2, 0, 1, 3)
    received = lax.all_to_all(advected, "tile", split_axis=0, concat_axis=0, tiled=True)
    band_count = band_table.shape[0]
    inverse = diffusion[0]
    diffused = jnp.einsum("kl,itly->tkiy", inverse, received, preferred_element_type=jnp.float32)
    diffused16 = diffused.astype(jnp.bfloat16)
    picked = (jnp.arange(band_count, dtype=jnp.int32) == band[0])[:, None, None]
    radiation = jnp.sum(jnp.where(picked, band_table, jnp.zeros_like(band_table)), axis=0)
    heating = jnp.einsum("kl,tlxy->tkxy", radiation, diffused16, preferred_element_type=jnp.float32)
    return (diffused + heating).astype(jnp.bfloat16)


def solution(mesh):
    placed = (
        P(None, None, "sec", "tile"),
        P(None, None, "sec", "tile"),
        P(("sec", "tile"), None),
        P(("sec", "tile"), None, None),
        P(("sec", "tile")),
        P(),
    )
    return jax.shard_map(
        per_device,
        mesh=mesh,
        in_specs=placed,
        out_specs=P(None, None, ("sec", "tile"), None),
        check_vma=False,
    )
```

```python
import functools

import jax
import jax.numpy as jnp
from jax import lax
from jax.experimental import pallas as pl
from jax.experimental.pallas import tpu as pltpu
from jax.sharding import PartitionSpec as P

STEPS = 3


def stencil_kernel(step, emit, last, *refs):
    if step:
        q_ref, wind_ref, north_ref, south_ref, east_ref, west_ref = refs[:6]
        refs = refs[6:]
    else:
        q_ref = refs[0]
        refs = refs[1:]
    if step:
        out_ref = refs[0]
        refs = refs[1:]
    if emit:
        top_ref, bottom_ref, first_ref, last_ref = refs[:4]
        refs = refs[4:]
    new_scr, row_scr = refs

    count, levels, rows, cols = q_ref.shape
    planes = levels * rows

    if step:
        cx = wind_ref[0].astype(jnp.float32)
        cy = wind_ref[1].astype(jnp.float32)
        half_x = 0.5 * cx
        full_x = half_x * cx
        half_y = 0.5 * cy
        full_y = half_y * cy
        strips = jnp.zeros((cols, count * planes), jnp.float32)
        strips = jnp.where(
            lax.broadcasted_iota(jnp.int32, strips.shape, 0) == 0,
            east_ref[...].astype(jnp.float32),
            jnp.where(
                lax.broadcasted_iota(jnp.int32, strips.shape, 0) == 1,
                west_ref[...].astype(jnp.float32),
                strips,
            ),
        )
        columns = strips.T
        sub = lax.broadcasted_iota(jnp.int32, (levels, rows, cols), 1)
        lane = lax.broadcasted_iota(jnp.int32, (levels, rows, cols), 2)

    for field in range(count):
        centre = q_ref[field].astype(jnp.float32)
        if step:
            row_scr[:, rows - 1, :] = north_ref[field].astype(jnp.float32)
            north_halo = row_scr[...]
            row_scr[:, 0, :] = south_ref[field].astype(jnp.float32)
            south_halo = row_scr[...]
            north = jnp.where(sub == rows - 1, north_halo, pltpu.roll(centre, rows - 1, 1))
            south = jnp.where(sub == 0, south_halo, pltpu.roll(centre, 1, 1))
            side = columns[field * planes:(field + 1) * planes].reshape(levels, rows, cols)
            side = pltpu.roll(side, cols - 1, 2)
            east = jnp.where(lane == cols - 1, side, pltpu.roll(centre, cols - 1, 2))
            west = jnp.where(lane == 0, side, pltpu.roll(centre, 1, 2))
            out = centre - half_x * (north - south) + full_x * (north - 2.0 * centre + south)
            out = out - half_y * (east - west) + full_y * (east - 2.0 * centre + west)
            new = out.astype(jnp.bfloat16)
            if last:
                new_scr[...] = new.astype(jnp.float32)
                for row in range(rows):
                    out_ref[row, field] = new_scr[:, row, :].astype(out_ref.dtype)
            else:
                out_ref[field] = new
        else:
            new = q_ref[field]
        if emit:
            new_scr[...] = new.astype(jnp.float32)
            top_ref[field] = new_scr[:, 0, :].astype(top_ref.dtype)
            bottom_ref[field] = new_scr[:, rows - 1, :].astype(bottom_ref.dtype)
            flat = new.astype(jnp.float32).reshape(planes, cols).astype(jnp.bfloat16)
            pick = lax.broadcasted_iota(jnp.int32, (8, cols), 1)
            which = lax.broadcasted_iota(jnp.int32, (8, cols), 0)
            onehot = jnp.where(
                ((which == 0) & (pick == 0)) | ((which == 1) & (pick == cols - 1)), 1.0, 0.0
            ).astype(jnp.bfloat16)
            edges = lax.dot_general(
                onehot, flat, (((1,), (1,)), ((), ())), preferred_element_type=jnp.float32
            )
            first_ref[:, field * planes:(field + 1) * planes] = edges[0:1].astype(first_ref.dtype)
            last_ref[:, field * planes:(field + 1) * planes] = edges[1:2].astype(last_ref.dtype)


def stencil_call(step, emit, q, *extra, order=None):
    count, levels, rows, cols = q.shape
    planes = levels * rows
    last = order is not None
    outs = []
    if last:
        outs.append(jax.ShapeDtypeStruct((rows, count, levels, cols), q.dtype))
    elif step:
        outs.append(jax.ShapeDtypeStruct(q.shape, q.dtype))
    if emit:
        outs += [
            jax.ShapeDtypeStruct((count, levels, cols), q.dtype),
            jax.ShapeDtypeStruct((count, levels, cols), q.dtype),
            jax.ShapeDtypeStruct((1, count * planes), q.dtype),
            jax.ShapeDtypeStruct((1, count * planes), q.dtype),
        ]
    vmem = pl.BlockSpec(memory_space=pltpu.VMEM)
    ins = [vmem] * (1 + len(extra))
    operands = (q,) + extra
    return pl.pallas_call(
        functools.partial(stencil_kernel, step, emit, last),
        out_shape=tuple(outs),
        in_specs=ins,
        out_specs=tuple([vmem] * len(outs)),
        scratch_shapes=[
            pltpu.VMEM((levels, rows, cols), jnp.float32),
            pltpu.VMEM((levels, rows, cols), jnp.float32),
        ],
    )(*operands)


def exchange(top, bottom, first, last):
    sec = lax.axis_size("sec")
    tile = lax.axis_size("tile")
    north = lax.ppermute(top, "sec", [(i, (i - 1) % sec) for i in range(sec)])
    south = lax.ppermute(bottom, "sec", [(i, (i + 1) % sec) for i in range(sec)])
    east = lax.ppermute(first, "tile", [(i, (i - 1) % tile) for i in range(tile)])
    west = lax.ppermute(last, "tile", [(i, (i + 1) % tile) for i in range(tile)])
    return north, south, east, west


def per_device(tracers, courant, destination, diffusion, band, band_table):
    order = jnp.argsort(destination[0]).astype(jnp.int32)
    halos = stencil_call(0, True, tracers)
    advected = tracers
    for step in range(STEPS):
        emit = step < STEPS - 1
        final = None if emit or tracers.shape[2] > 8 else order
        result = stencil_call(1, emit, advected, courant, *exchange(*halos), order=final)
        advected = result[0]
        halos = result[1:]
    if tracers.shape[2] > 8:
        advected = advected.transpose(2, 0, 1, 3)
    advected = jnp.take(advected, order, axis=0)
    received = lax.all_to_all(advected, "tile", split_axis=0, concat_axis=0, tiled=True)
    band_count = band_table.shape[0]
    inverse = diffusion[0]
    diffused = jnp.einsum("kl,itly->tkiy", inverse, received, preferred_element_type=jnp.float32)
    diffused16 = diffused.astype(jnp.bfloat16)
    picked = (jnp.arange(band_count, dtype=jnp.int32) == band[0])[:, None, None]
    radiation = jnp.sum(jnp.where(picked, band_table, jnp.zeros_like(band_table)), axis=0)
    heating = jnp.einsum("kl,tlxy->tkxy", radiation, diffused16, preferred_element_type=jnp.float32)
    return (diffused + heating).astype(jnp.bfloat16)


def solution(mesh):
    placed = (
        P(None, None, "sec", "tile"),
        P(None, None, "sec", "tile"),
        P(("sec", "tile"), None),
        P(("sec", "tile"), None, None),
        P(("sec", "tile")),
        P(),
    )
    return jax.shard_map(
        per_device,
        mesh=mesh,
        in_specs=placed,
        out_specs=P(None, None, ("sec", "tile"), None),
        check_vma=False,
    )
```

```python
import functools

import jax
import jax.numpy as jnp
from jax import lax
from jax.experimental import pallas as pl
from jax.experimental.pallas import tpu as pltpu
from jax.sharding import PartitionSpec as P

STEPS = 3


LEVEL_BLOCK = 8


def stencil_kernel(step, emit, *refs):
    if step:
        q_ref, wind_ref, north_ref, south_ref, east_ref, west_ref = refs[:6]
        refs = refs[6:]
    else:
        q_ref = refs[0]
        refs = refs[1:]
    if step:
        out_ref = refs[0]
        refs = refs[1:]
    if emit:
        top_ref, bottom_ref, first_ref, last_ref = refs[:4]
        refs = refs[4:]
    new_scr, row_scr, halo_scr, side_scr = refs

    count, levels, rows, cols = q_ref.shape
    planes = levels * rows
    block = LEVEL_BLOCK if levels % LEVEL_BLOCK == 0 else 1

    if step:
        strips = jnp.zeros((cols, count * planes), jnp.float32)
        strips = jnp.where(
            lax.broadcasted_iota(jnp.int32, strips.shape, 0) == 0,
            east_ref[...].astype(jnp.float32),
            jnp.where(
                lax.broadcasted_iota(jnp.int32, strips.shape, 0) == 1,
                west_ref[...].astype(jnp.float32),
                strips,
            ),
        )
        side_scr[...] = strips.T
        halo_scr[0] = north_ref[...].astype(jnp.float32)
        halo_scr[1] = south_ref[...].astype(jnp.float32)
        sub = lax.broadcasted_iota(jnp.int32, (block, rows, cols), 1)
        lane = lax.broadcasted_iota(jnp.int32, (block, rows, cols), 2)

    for field in range(count):
        if step:
            def body(index, carry):
                first = pl.multiple_of(index * block, block)
                levels_here = pl.ds(first, block)
                centre = q_ref[field, levels_here].astype(jnp.float32)
                cx = wind_ref[0, levels_here].astype(jnp.float32)
                cy = wind_ref[1, levels_here].astype(jnp.float32)
                half_x = 0.5 * cx
                full_x = half_x * cx
                half_y = 0.5 * cy
                full_y = half_y * cy
                row_scr[:, rows - 1, :] = halo_scr[0, field, levels_here]
                north = jnp.where(sub == rows - 1, row_scr[...], pltpu.roll(centre, rows - 1, 1))
                row_scr[:, 0, :] = halo_scr[1, field, levels_here]
                south = jnp.where(sub == 0, row_scr[...], pltpu.roll(centre, 1, 1))
                offset = pl.multiple_of(field * planes + first * rows, 8)
                side = side_scr[pl.ds(offset, block * rows)].reshape(block, rows, cols)
                side = pltpu.roll(side, cols - 1, 2)
                east = jnp.where(lane == cols - 1, side, pltpu.roll(centre, cols - 1, 2))
                west = jnp.where(lane == 0, side, pltpu.roll(centre, 1, 2))
                out = centre - half_x * (north - south) + full_x * (north - 2.0 * centre + south)
                out = out - half_y * (east - west) + full_y * (east - 2.0 * centre + west)
                new = out.astype(jnp.bfloat16)
                out_ref[field, levels_here] = new
                if emit:
                    new_scr[levels_here] = new.astype(jnp.float32)
                return carry

            lax.fori_loop(0, levels // block, body, 0)
        elif emit:
            new_scr[...] = q_ref[field].astype(jnp.float32)
        if emit:
            top_ref[field] = new_scr[:, 0, :].astype(top_ref.dtype)
            bottom_ref[field] = new_scr[:, rows - 1, :].astype(bottom_ref.dtype)
            flat = new_scr[...].reshape(planes, cols).astype(jnp.bfloat16)
            pick = lax.broadcasted_iota(jnp.int32, (8, cols), 1)
            which = lax.broadcasted_iota(jnp.int32, (8, cols), 0)
            onehot = jnp.where(
                ((which == 0) & (pick == 0)) | ((which == 1) & (pick == cols - 1)), 1.0, 0.0
            ).astype(jnp.bfloat16)
            edges = lax.dot_general(
                onehot, flat, (((1,), (1,)), ((), ())), preferred_element_type=jnp.float32
            )
            first_ref[:, field * planes:(field + 1) * planes] = edges[0:1].astype(first_ref.dtype)
            last_ref[:, field * planes:(field + 1) * planes] = edges[1:2].astype(last_ref.dtype)


def stencil_call(step, emit, q, *extra):
    count, levels, rows, cols = q.shape
    planes = levels * rows
    outs = []
    if step:
        outs.append(jax.ShapeDtypeStruct(q.shape, q.dtype))
    if emit:
        outs += [
            jax.ShapeDtypeStruct((count, levels, cols), q.dtype),
            jax.ShapeDtypeStruct((count, levels, cols), q.dtype),
            jax.ShapeDtypeStruct((1, count * planes), q.dtype),
            jax.ShapeDtypeStruct((1, count * planes), q.dtype),
        ]
    vmem = pl.BlockSpec(memory_space=pltpu.VMEM)
    return pl.pallas_call(
        functools.partial(stencil_kernel, step, emit),
        out_shape=tuple(outs),
        in_specs=[vmem] * (1 + len(extra)),
        out_specs=tuple([vmem] * len(outs)),
        scratch_shapes=[
            pltpu.VMEM((levels, rows, cols), jnp.float32),
            pltpu.VMEM((LEVEL_BLOCK, rows, cols), jnp.float32),
            pltpu.VMEM((2, count, levels, cols), jnp.float32),
            pltpu.VMEM((count * planes, cols), jnp.float32),
        ],
    )(q, *extra)


def exchange(top, bottom, first, last):
    sec = lax.axis_size("sec")
    tile = lax.axis_size("tile")
    north = lax.ppermute(top, "sec", [(i, (i - 1) % sec) for i in range(sec)])
    south = lax.ppermute(bottom, "sec", [(i, (i + 1) % sec) for i in range(sec)])
    east = lax.ppermute(first, "tile", [(i, (i - 1) % tile) for i in range(tile)])
    west = lax.ppermute(last, "tile", [(i, (i + 1) % tile) for i in range(tile)])
    return north, south, east, west


def per_device(tracers, courant, destination, diffusion, band, band_table):
    halos = stencil_call(0, True, tracers)
    advected = tracers
    for step in range(STEPS):
        emit = step < STEPS - 1
        result = stencil_call(1, emit, advected, courant, *exchange(*halos))
        advected = result[0]
        halos = result[1:]
    order = jnp.argsort(destination[0])
    band_count = band_table.shape[0]
    ordered = jnp.take(advected, order, axis=2)
    received = lax.all_to_all(ordered, "tile", split_axis=2, concat_axis=2, tiled=True)
    inverse = diffusion[0]
    diffused = jnp.einsum("kl,tlxy->tkxy", inverse, received, preferred_element_type=jnp.float32)
    diffused16 = diffused.astype(jnp.bfloat16)
    picked = (jnp.arange(band_count, dtype=jnp.int32) == band[0])[:, None, None]
    radiation = jnp.sum(jnp.where(picked, band_table, jnp.zeros_like(band_table)), axis=0)
    heating = jnp.einsum("kl,tlxy->tkxy", radiation, diffused16, preferred_element_type=jnp.float32)
    return (diffused + heating).astype(jnp.bfloat16)


def solution(mesh):
    placed = (
        P(None, None, "sec", "tile"),
        P(None, None, "sec", "tile"),
        P(("sec", "tile"), None),
        P(("sec", "tile"), None, None),
        P(("sec", "tile")),
        P(),
    )
    return jax.shard_map(
        per_device,
        mesh=mesh,
        in_specs=placed,
        out_specs=P(None, None, ("sec", "tile"), None),
        check_vma=False,
    )
```

```python
import functools

import jax
import jax.numpy as jnp
from jax import lax
from jax.experimental import pallas as pl
from jax.experimental.pallas import tpu as pltpu
from jax.sharding import PartitionSpec as P

STEPS = 3


LEVEL_BLOCK = 8


def stencil_kernel(step, emit, *refs):
    if step:
        q_ref, wind_ref, north_ref, south_ref, east_ref, west_ref = refs[:6]
        refs = refs[6:]
    else:
        q_ref = refs[0]
        refs = refs[1:]
    if step:
        out_ref = refs[0]
        refs = refs[1:]
    if emit:
        top_ref, bottom_ref, first_ref, last_ref = refs[:4]
        refs = refs[4:]
    new_scr, row_scr, halo_scr, side_scr, factor_scr = refs

    count, levels, rows, cols = q_ref.shape
    planes = levels * rows
    block = LEVEL_BLOCK if levels % LEVEL_BLOCK == 0 else 1

    if step:
        strips = jnp.zeros((cols, count * planes), jnp.float32)
        strips = jnp.where(
            lax.broadcasted_iota(jnp.int32, strips.shape, 0) == 0,
            east_ref[...].astype(jnp.float32),
            jnp.where(
                lax.broadcasted_iota(jnp.int32, strips.shape, 0) == 1,
                west_ref[...].astype(jnp.float32),
                strips,
            ),
        )
        side_scr[...] = strips.T
        halo_scr[0] = north_ref[...].astype(jnp.float32)
        halo_scr[1] = south_ref[...].astype(jnp.float32)
        sub = lax.broadcasted_iota(jnp.int32, (block, rows, cols), 1)
        lane = lax.broadcasted_iota(jnp.int32, (block, rows, cols), 2)
        for index in range(levels // block):
            levels_here = pl.ds(index * block, block)
            cx = wind_ref[0, levels_here].astype(jnp.float32)
            cy = wind_ref[1, levels_here].astype(jnp.float32)
            half_x = 0.5 * cx
            half_y = 0.5 * cy
            factor_scr[0, levels_here] = half_x
            factor_scr[1, levels_here] = half_x * cx
            factor_scr[2, levels_here] = half_y
            factor_scr[3, levels_here] = half_y * cy

    for field in range(count):
        if step:
            for index in range(levels // block):
                first = index * block
                levels_here = pl.ds(first, block)
                centre = q_ref[field, levels_here].astype(jnp.float32)
                half_x = factor_scr[0, levels_here]
                full_x = factor_scr[1, levels_here]
                half_y = factor_scr[2, levels_here]
                full_y = factor_scr[3, levels_here]
                row_scr[:, rows - 1, :] = halo_scr[0, field, levels_here]
                north = jnp.where(sub == rows - 1, row_scr[...], pltpu.roll(centre, rows - 1, 1))
                row_scr[:, 0, :] = halo_scr[1, field, levels_here]
                south = jnp.where(sub == 0, row_scr[...], pltpu.roll(centre, 1, 1))
                offset = field * planes + first * rows
                side = side_scr[pl.ds(offset, block * rows)].reshape(block, rows, cols)
                side = pltpu.roll(side, cols - 1, 2)
                east = jnp.where(lane == cols - 1, side, pltpu.roll(centre, cols - 1, 2))
                west = jnp.where(lane == 0, side, pltpu.roll(centre, 1, 2))
                out = centre - half_x * (north - south) + full_x * (north - 2.0 * centre + south)
                out = out - half_y * (east - west) + full_y * (east - 2.0 * centre + west)
                new = out.astype(jnp.bfloat16)
                out_ref[field, levels_here] = new
                if emit:
                    new_scr[levels_here] = new.astype(jnp.float32)
        elif emit:
            new_scr[...] = q_ref[field].astype(jnp.float32)
        if emit:
            top_ref[field] = new_scr[:, 0, :].astype(top_ref.dtype)
            bottom_ref[field] = new_scr[:, rows - 1, :].astype(bottom_ref.dtype)
            flat = new_scr[...].reshape(planes, cols).astype(jnp.bfloat16)
            pick = lax.broadcasted_iota(jnp.int32, (8, cols), 1)
            which = lax.broadcasted_iota(jnp.int32, (8, cols), 0)
            onehot = jnp.where(
                ((which == 0) & (pick == 0)) | ((which == 1) & (pick == cols - 1)), 1.0, 0.0
            ).astype(jnp.bfloat16)
            edges = lax.dot_general(
                onehot, flat, (((1,), (1,)), ((), ())), preferred_element_type=jnp.float32
            )
            first_ref[:, field * planes:(field + 1) * planes] = edges[0:1].astype(first_ref.dtype)
            last_ref[:, field * planes:(field + 1) * planes] = edges[1:2].astype(last_ref.dtype)


def stencil_call(step, emit, q, *extra):
    count, levels, rows, cols = q.shape
    planes = levels * rows
    outs = []
    if step:
        outs.append(jax.ShapeDtypeStruct(q.shape, q.dtype))
    if emit:
        outs += [
            jax.ShapeDtypeStruct((count, levels, cols), q.dtype),
            jax.ShapeDtypeStruct((count, levels, cols), q.dtype),
            jax.ShapeDtypeStruct((1, count * planes), q.dtype),
            jax.ShapeDtypeStruct((1, count * planes), q.dtype),
        ]
    vmem = pl.BlockSpec(memory_space=pltpu.VMEM)
    return pl.pallas_call(
        functools.partial(stencil_kernel, step, emit),
        out_shape=tuple(outs),
        in_specs=[vmem] * (1 + len(extra)),
        out_specs=tuple([vmem] * len(outs)),
        scratch_shapes=[
            pltpu.VMEM((levels, rows, cols), jnp.float32),
            pltpu.VMEM((LEVEL_BLOCK, rows, cols), jnp.float32),
            pltpu.VMEM((2, count, levels, cols), jnp.float32),
            pltpu.VMEM((count * planes, cols), jnp.float32),
            pltpu.VMEM((4, levels, rows, cols), jnp.float32),
        ],
    )(q, *extra)


def exchange(top, bottom, first, last):
    sec = lax.axis_size("sec")
    tile = lax.axis_size("tile")
    north = lax.ppermute(top, "sec", [(i, (i - 1) % sec) for i in range(sec)])
    south = lax.ppermute(bottom, "sec", [(i, (i + 1) % sec) for i in range(sec)])
    east = lax.ppermute(first, "tile", [(i, (i - 1) % tile) for i in range(tile)])
    west = lax.ppermute(last, "tile", [(i, (i + 1) % tile) for i in range(tile)])
    return north, south, east, west


def per_device(tracers, courant, destination, diffusion, band, band_table):
    halos = stencil_call(0, True, tracers)
    advected = tracers
    for step in range(STEPS):
        emit = step < STEPS - 1
        result = stencil_call(1, emit, advected, courant, *exchange(*halos))
        advected = result[0]
        halos = result[1:]
    order = jnp.argsort(destination[0])
    band_count = band_table.shape[0]
    ordered = jnp.take(advected, order, axis=2)
    received = lax.all_to_all(ordered, "tile", split_axis=2, concat_axis=2, tiled=True)
    inverse = diffusion[0]
    diffused = jnp.einsum("kl,tlxy->tkxy", inverse, received, preferred_element_type=jnp.float32)
    diffused16 = diffused.astype(jnp.bfloat16)
    picked = (jnp.arange(band_count, dtype=jnp.int32) == band[0])[:, None, None]
    radiation = jnp.sum(jnp.where(picked, band_table, jnp.zeros_like(band_table)), axis=0)
    heating = jnp.einsum("kl,tlxy->tkxy", radiation, diffused16, preferred_element_type=jnp.float32)
    return (diffused + heating).astype(jnp.bfloat16)


def solution(mesh):
    placed = (
        P(None, None, "sec", "tile"),
        P(None, None, "sec", "tile"),
        P(("sec", "tile"), None),
        P(("sec", "tile"), None, None),
        P(("sec", "tile")),
        P(),
    )
    return jax.shard_map(
        per_device,
        mesh=mesh,
        in_specs=placed,
        out_specs=P(None, None, ("sec", "tile"), None),
        check_vma=False,
    )
```

```python
import functools

import jax
import jax.numpy as jnp
from jax import lax
from jax.experimental import pallas as pl
from jax.experimental.pallas import tpu as pltpu
from jax.sharding import PartitionSpec as P

STEPS = 3


LEVEL_BLOCK = 8


def stencil_kernel(step, emit, *refs):
    if step:
        q_ref, wind_ref, north_ref, south_ref, east_ref, west_ref = refs[:6]
        refs = refs[6:]
    else:
        q_ref = refs[0]
        refs = refs[1:]
    if step:
        out_ref = refs[0]
        refs = refs[1:]
    if emit:
        top_ref, bottom_ref, first_ref, last_ref = refs[:4]
        refs = refs[4:]
    new_scr, row_scr, halo_scr, side_scr, factor_scr = refs

    count, levels, rows, cols = q_ref.shape
    planes = levels * rows
    block = LEVEL_BLOCK if levels % LEVEL_BLOCK == 0 else 1

    if step:
        strips = jnp.zeros((cols, count * planes), jnp.float32)
        strips = jnp.where(
            lax.broadcasted_iota(jnp.int32, strips.shape, 0) == 0,
            east_ref[...].astype(jnp.float32),
            jnp.where(
                lax.broadcasted_iota(jnp.int32, strips.shape, 0) == 1,
                west_ref[...].astype(jnp.float32),
                strips,
            ),
        )
        side_scr[...] = strips.T
        halo_scr[0] = north_ref[...].astype(jnp.float32)
        halo_scr[1] = south_ref[...].astype(jnp.float32)
        sub = lax.broadcasted_iota(jnp.int32, (block, rows, cols), 1)
        lane = lax.broadcasted_iota(jnp.int32, (block, rows, cols), 2)
        for index in range(levels // block):
            levels_here = pl.ds(index * block, block)
            cx = wind_ref[0, levels_here].astype(jnp.float32)
            cy = wind_ref[1, levels_here].astype(jnp.float32)
            half_x = 0.5 * cx
            half_y = 0.5 * cy
            factor_scr[0, levels_here] = half_x
            factor_scr[1, levels_here] = half_x * cx
            factor_scr[2, levels_here] = half_y
            factor_scr[3, levels_here] = half_y * cy

    for field in range(count):
        if step:
            for index in range(levels // block):
                first = index * block
                levels_here = pl.ds(first, block)
                centre = q_ref[field, levels_here].astype(jnp.float32)
                half_x = factor_scr[0, levels_here]
                full_x = factor_scr[1, levels_here]
                half_y = factor_scr[2, levels_here]
                full_y = factor_scr[3, levels_here]
                row_scr[:, rows - 1, :] = halo_scr[0, field, levels_here]
                north = jnp.where(sub == rows - 1, row_scr[...], pltpu.roll(centre, rows - 1, 1))
                row_scr[:, 0, :] = halo_scr[1, field, levels_here]
                south = jnp.where(sub == 0, row_scr[...], pltpu.roll(centre, 1, 1))
                offset = field * planes + first * rows
                side = side_scr[pl.ds(offset, block * rows)].reshape(block, rows, cols)
                side = pltpu.roll(side, cols - 1, 2)
                east = jnp.where(lane == cols - 1, side, pltpu.roll(centre, cols - 1, 2))
                west = jnp.where(lane == 0, side, pltpu.roll(centre, 1, 2))
                out = centre - half_x * (north - south) + full_x * (north - 2.0 * centre + south)
                out = out - half_y * (east - west) + full_y * (east - 2.0 * centre + west)
                new = out.astype(jnp.bfloat16)
                out_ref[field, levels_here] = new
                if emit:
                    new_scr[levels_here] = new.astype(jnp.float32)
        elif emit:
            new_scr[...] = q_ref[field].astype(jnp.float32)
        if emit:
            top_ref[field] = new_scr[:, 0, :].astype(top_ref.dtype)
            bottom_ref[field] = new_scr[:, rows - 1, :].astype(bottom_ref.dtype)
            flat = new_scr[...].reshape(planes, cols).astype(jnp.bfloat16)
            pick = lax.broadcasted_iota(jnp.int32, (8, cols), 1)
            which = lax.broadcasted_iota(jnp.int32, (8, cols), 0)
            onehot = jnp.where(
                ((which == 0) & (pick == 0)) | ((which == 1) & (pick == cols - 1)), 1.0, 0.0
            ).astype(jnp.bfloat16)
            edges = lax.dot_general(
                onehot, flat, (((1,), (1,)), ((), ())), preferred_element_type=jnp.float32
            )
            first_ref[:, field * planes:(field + 1) * planes] = edges[0:1].astype(first_ref.dtype)
            last_ref[:, field * planes:(field + 1) * planes] = edges[1:2].astype(last_ref.dtype)


def stencil_call(step, emit, q, *extra):
    count, levels, rows, cols = q.shape
    planes = levels * rows
    outs = []
    if step:
        outs.append(jax.ShapeDtypeStruct(q.shape, q.dtype))
    if emit:
        outs += [
            jax.ShapeDtypeStruct((count, levels, cols), q.dtype),
            jax.ShapeDtypeStruct((count, levels, cols), q.dtype),
            jax.ShapeDtypeStruct((1, count * planes), q.dtype),
            jax.ShapeDtypeStruct((1, count * planes), q.dtype),
        ]
    vmem = pl.BlockSpec(memory_space=pltpu.VMEM)
    return pl.pallas_call(
        functools.partial(stencil_kernel, step, emit),
        out_shape=tuple(outs),
        in_specs=[vmem] * (1 + len(extra)),
        out_specs=tuple([vmem] * len(outs)),
        scratch_shapes=[
            pltpu.VMEM((levels, rows, cols), jnp.float32),
            pltpu.VMEM((LEVEL_BLOCK, rows, cols), jnp.float32),
            pltpu.VMEM((2, count, levels, cols), jnp.float32),
            pltpu.VMEM((count * planes, cols), jnp.float32),
            pltpu.VMEM((4, levels, rows, cols), jnp.float32),
        ],
    )(q, *extra)


def exchange(top, bottom, first, last):
    sec = lax.axis_size("sec")
    tile = lax.axis_size("tile")
    north = lax.ppermute(top, "sec", [(i, (i - 1) % sec) for i in range(sec)])
    south = lax.ppermute(bottom, "sec", [(i, (i + 1) % sec) for i in range(sec)])
    east = lax.ppermute(first, "tile", [(i, (i - 1) % tile) for i in range(tile)])
    west = lax.ppermute(last, "tile", [(i, (i + 1) % tile) for i in range(tile)])
    return north, south, east, west


def per_device(tracers, courant, destination, diffusion, band, band_table):
    halos = stencil_call(0, True, tracers)
    advected = tracers
    for step in range(STEPS):
        emit = step < STEPS - 1
        result = stencil_call(1, emit, advected, courant, *exchange(*halos))
        advected = result[0]
        halos = result[1:]
    order = jnp.argsort(destination[0])
    band_count = band_table.shape[0]
    ordered = jnp.take(advected, order, axis=2, mode="clip")
    received = lax.all_to_all(ordered, "tile", split_axis=2, concat_axis=2, tiled=True)
    inverse = diffusion[0]
    diffused = jnp.einsum("kl,tlxy->tkxy", inverse, received, preferred_element_type=jnp.float32)
    diffused16 = diffused.astype(jnp.bfloat16)
    picked = (jnp.arange(band_count, dtype=jnp.int32) == band[0])[:, None, None]
    radiation = jnp.sum(jnp.where(picked, band_table, jnp.zeros_like(band_table)), axis=0)
    heating = jnp.einsum("kl,tlxy->tkxy", radiation, diffused16, preferred_element_type=jnp.float32)
    return (diffused + heating).astype(jnp.bfloat16)


def solution(mesh):
    placed = (
        P(None, None, "sec", "tile"),
        P(None, None, "sec", "tile"),
        P(("sec", "tile"), None),
        P(("sec", "tile"), None, None),
        P(("sec", "tile")),
        P(),
    )
    return jax.shard_map(
        per_device,
        mesh=mesh,
        in_specs=placed,
        out_specs=P(None, None, ("sec", "tile"), None),
        check_vma=False,
    )
```

```python
import functools

import jax
import jax.numpy as jnp
from jax import lax
from jax.experimental import pallas as pl
from jax.experimental.pallas import tpu as pltpu
from jax.sharding import PartitionSpec as P

STEPS = 3


LEVEL_BLOCK = 8


def stencil_kernel(step, emit, *refs):
    if step:
        q_ref, wind_ref, north_ref, south_ref, east_ref, west_ref = refs[:6]
        refs = refs[6:]
    else:
        q_ref = refs[0]
        refs = refs[1:]
    if step:
        out_ref = refs[0]
        refs = refs[1:]
    if emit:
        top_ref, bottom_ref, first_ref, last_ref = refs[:4]
        refs = refs[4:]
    new_scr, row_scr, halo_scr, side_scr, factor_scr = refs

    count, levels, rows, cols = q_ref.shape
    planes = levels * rows
    block = LEVEL_BLOCK if levels % LEVEL_BLOCK == 0 else 1

    if step:
        strips = jnp.zeros((cols, count * planes), jnp.float32)
        strips = jnp.where(
            lax.broadcasted_iota(jnp.int32, strips.shape, 0) == 0,
            east_ref[...].astype(jnp.float32),
            jnp.where(
                lax.broadcasted_iota(jnp.int32, strips.shape, 0) == 1,
                west_ref[...].astype(jnp.float32),
                strips,
            ),
        )
        side_scr[...] = strips.T
        halo_scr[0] = north_ref[...].astype(jnp.float32)
        halo_scr[1] = south_ref[...].astype(jnp.float32)
        sub = lax.broadcasted_iota(jnp.int32, (block, rows, cols), 1)
        lane = lax.broadcasted_iota(jnp.int32, (block, rows, cols), 2)
        for index in range(levels // block):
            levels_here = pl.ds(index * block, block)
            cx = wind_ref[0, levels_here].astype(jnp.float32)
            cy = wind_ref[1, levels_here].astype(jnp.float32)
            half_x = 0.5 * cx
            half_y = 0.5 * cy
            factor_scr[0, levels_here] = half_x
            factor_scr[1, levels_here] = half_x * cx
            factor_scr[2, levels_here] = half_y
            factor_scr[3, levels_here] = half_y * cy

    for field in range(count):
        if step:
            for index in range(levels // block):
                first = index * block
                levels_here = pl.ds(first, block)
                centre = q_ref[field, levels_here].astype(jnp.float32)
                half_x = factor_scr[0, levels_here]
                full_x = factor_scr[1, levels_here]
                half_y = factor_scr[2, levels_here]
                full_y = factor_scr[3, levels_here]
                row_scr[:, rows - 1, :] = halo_scr[0, field, levels_here]
                north = jnp.where(sub == rows - 1, row_scr[...], pltpu.roll(centre, rows - 1, 1))
                row_scr[:, 0, :] = halo_scr[1, field, levels_here]
                south = jnp.where(sub == 0, row_scr[...], pltpu.roll(centre, 1, 1))
                offset = field * planes + first * rows
                side = side_scr[pl.ds(offset, block * rows)].reshape(block, rows, cols)
                side = pltpu.roll(side, cols - 1, 2)
                east = jnp.where(lane == cols - 1, side, pltpu.roll(centre, cols - 1, 2))
                west = jnp.where(lane == 0, side, pltpu.roll(centre, 1, 2))
                out = centre - half_x * (north - south) + full_x * (north - 2.0 * centre + south)
                out = out - half_y * (east - west) + full_y * (east - 2.0 * centre + west)
                new = out.astype(jnp.bfloat16)
                out_ref[field, levels_here] = new
                if emit:
                    new_scr[levels_here] = new.astype(jnp.float32)
        elif emit:
            new_scr[...] = q_ref[field].astype(jnp.float32)
        if emit:
            top_ref[field] = new_scr[:, 0, :].astype(top_ref.dtype)
            bottom_ref[field] = new_scr[:, rows - 1, :].astype(bottom_ref.dtype)
            flat = new_scr[...].reshape(planes, cols).astype(jnp.bfloat16)
            pick = lax.broadcasted_iota(jnp.int32, (8, cols), 1)
            which = lax.broadcasted_iota(jnp.int32, (8, cols), 0)
            onehot = jnp.where(
                ((which == 0) & (pick == 0)) | ((which == 1) & (pick == cols - 1)), 1.0, 0.0
            ).astype(jnp.bfloat16)
            edges = lax.dot_general(
                onehot, flat, (((1,), (1,)), ((), ())), preferred_element_type=jnp.float32
            )
            first_ref[:, field * planes:(field + 1) * planes] = edges[0:1].astype(first_ref.dtype)
            last_ref[:, field * planes:(field + 1) * planes] = edges[1:2].astype(last_ref.dtype)


def stencil_call(step, emit, q, *extra):
    count, levels, rows, cols = q.shape
    planes = levels * rows
    outs = []
    if step:
        outs.append(jax.ShapeDtypeStruct(q.shape, q.dtype))
    if emit:
        outs += [
            jax.ShapeDtypeStruct((count, levels, cols), q.dtype),
            jax.ShapeDtypeStruct((count, levels, cols), q.dtype),
            jax.ShapeDtypeStruct((1, count * planes), q.dtype),
            jax.ShapeDtypeStruct((1, count * planes), q.dtype),
        ]
    vmem = pl.BlockSpec(memory_space=pltpu.VMEM)
    return pl.pallas_call(
        functools.partial(stencil_kernel, step, emit),
        out_shape=tuple(outs),
        in_specs=[vmem] * (1 + len(extra)),
        out_specs=tuple([vmem] * len(outs)),
        scratch_shapes=[
            pltpu.VMEM((levels, rows, cols), jnp.float32),
            pltpu.VMEM((LEVEL_BLOCK, rows, cols), jnp.float32),
            pltpu.VMEM((2, count, levels, cols), jnp.float32),
            pltpu.VMEM((count * planes, cols), jnp.float32),
            pltpu.VMEM((4, levels, rows, cols), jnp.float32),
        ],
    )(q, *extra)


def exchange(top, bottom, first, last):
    sec = lax.axis_size("sec")
    tile = lax.axis_size("tile")
    north = lax.ppermute(top, "sec", [(i, (i - 1) % sec) for i in range(sec)])
    south = lax.ppermute(bottom, "sec", [(i, (i + 1) % sec) for i in range(sec)])
    east = lax.ppermute(first, "tile", [(i, (i - 1) % tile) for i in range(tile)])
    west = lax.ppermute(last, "tile", [(i, (i + 1) % tile) for i in range(tile)])
    return north, south, east, west


def per_device(tracers, courant, destination, diffusion, band, band_table):
    halos = stencil_call(0, True, tracers)
    halos = (tracers[:, :, 0, :], tracers[:, :, -1, :]) + tuple(halos[2:])
    advected = tracers
    for step in range(STEPS):
        emit = step < STEPS - 1
        result = stencil_call(1, emit, advected, courant, *exchange(*halos))
        advected = result[0]
        halos = result[1:]
    order = jnp.argsort(destination[0])
    band_count = band_table.shape[0]
    ordered = jnp.take(advected, order, axis=2, mode="clip")
    received = lax.all_to_all(ordered, "tile", split_axis=2, concat_axis=2, tiled=True)
    inverse = diffusion[0]
    diffused = jnp.einsum("kl,tlxy->tkxy", inverse, received, preferred_element_type=jnp.float32)
    diffused16 = diffused.astype(jnp.bfloat16)
    picked = (jnp.arange(band_count, dtype=jnp.int32) == band[0])[:, None, None]
    radiation = jnp.sum(jnp.where(picked, band_table, jnp.zeros_like(band_table)), axis=0)
    heating = jnp.einsum("kl,tlxy->tkxy", radiation, diffused16, preferred_element_type=jnp.float32)
    return (diffused + heating).astype(jnp.bfloat16)


def solution(mesh):
    placed = (
        P(None, None, "sec", "tile"),
        P(None, None, "sec", "tile"),
        P(("sec", "tile"), None),
        P(("sec", "tile"), None, None),
        P(("sec", "tile")),
        P(),
    )
    return jax.shard_map(
        per_device,
        mesh=mesh,
        in_specs=placed,
        out_specs=P(None, None, ("sec", "tile"), None),
        check_vma=False,
    )
```

```python
import functools

import jax
import jax.numpy as jnp
from jax import lax
from jax.experimental import pallas as pl
from jax.experimental.pallas import tpu as pltpu
from jax.sharding import PartitionSpec as P

STEPS = 3


LEVEL_BLOCK = 8


def stencil_kernel(step, emit, *refs):
    if step:
        q_ref, wind_ref, north_ref, south_ref, east_ref, west_ref = refs[:6]
        refs = refs[6:]
    else:
        q_ref = refs[0]
        refs = refs[1:]
    if step:
        out_ref = refs[0]
        refs = refs[1:]
    if emit:
        top_ref, bottom_ref, first_ref, last_ref = refs[:4]
        refs = refs[4:]
    new_scr, row_scr, halo_scr, side_scr, factor_scr = refs

    count, levels, rows, cols = q_ref.shape
    planes = levels * rows
    block = LEVEL_BLOCK if levels % LEVEL_BLOCK == 0 else 1

    if step:
        strips = jnp.zeros((cols, count * planes), jnp.float32)
        strips = jnp.where(
            lax.broadcasted_iota(jnp.int32, strips.shape, 0) == 0,
            east_ref[...].astype(jnp.float32),
            jnp.where(
                lax.broadcasted_iota(jnp.int32, strips.shape, 0) == 1,
                west_ref[...].astype(jnp.float32),
                strips,
            ),
        )
        side_scr[...] = strips.T
        halo_scr[0] = north_ref[...].astype(jnp.float32)
        halo_scr[1] = south_ref[...].astype(jnp.float32)
        sub = lax.broadcasted_iota(jnp.int32, (block, rows, cols), 1)
        lane = lax.broadcasted_iota(jnp.int32, (block, rows, cols), 2)
        for index in range(levels // block):
            levels_here = pl.ds(index * block, block)
            cx = wind_ref[0, levels_here].astype(jnp.float32)
            cy = wind_ref[1, levels_here].astype(jnp.float32)
            half_x = 0.5 * cx
            half_y = 0.5 * cy
            factor_scr[0, levels_here] = half_x
            factor_scr[1, levels_here] = half_x * cx
            factor_scr[2, levels_here] = half_y
            factor_scr[3, levels_here] = half_y * cy

    for field in range(count):
        if step:
            for index in range(levels // block):
                first = index * block
                levels_here = pl.ds(first, block)
                centre = q_ref[field, levels_here].astype(jnp.float32)
                half_x = factor_scr[0, levels_here]
                full_x = factor_scr[1, levels_here]
                half_y = factor_scr[2, levels_here]
                full_y = factor_scr[3, levels_here]
                row_scr[:, rows - 1, :] = halo_scr[0, field, levels_here]
                north = jnp.where(sub == rows - 1, row_scr[...], pltpu.roll(centre, rows - 1, 1))
                row_scr[:, 0, :] = halo_scr[1, field, levels_here]
                south = jnp.where(sub == 0, row_scr[...], pltpu.roll(centre, 1, 1))
                offset = field * planes + first * rows
                side = side_scr[pl.ds(offset, block * rows)].reshape(block, rows, cols)
                side = pltpu.roll(side, cols - 1, 2)
                east = jnp.where(lane == cols - 1, side, pltpu.roll(centre, cols - 1, 2))
                west = jnp.where(lane == 0, side, pltpu.roll(centre, 1, 2))
                out = centre - half_x * (north - south) + full_x * (north - 2.0 * centre + south)
                out = out - half_y * (east - west) + full_y * (east - 2.0 * centre + west)
                new = out.astype(jnp.bfloat16)
                out_ref[field, levels_here] = new
                if emit:
                    new_scr[levels_here] = new.astype(jnp.float32)
        elif emit:
            new_scr[...] = q_ref[field].astype(jnp.float32)
        if emit:
            top_ref[field] = new_scr[:, 0, :].astype(top_ref.dtype)
            bottom_ref[field] = new_scr[:, rows - 1, :].astype(bottom_ref.dtype)
            flat = new_scr[...].reshape(planes, cols).astype(jnp.bfloat16)
            pick = lax.broadcasted_iota(jnp.int32, (8, cols), 1)
            which = lax.broadcasted_iota(jnp.int32, (8, cols), 0)
            onehot = jnp.where(
                ((which == 0) & (pick == 0)) | ((which == 1) & (pick == cols - 1)), 1.0, 0.0
            ).astype(jnp.bfloat16)
            edges = lax.dot_general(
                onehot, flat, (((1,), (1,)), ((), ())), preferred_element_type=jnp.float32
            )
            first_ref[:, field * planes:(field + 1) * planes] = edges[0:1].astype(first_ref.dtype)
            last_ref[:, field * planes:(field + 1) * planes] = edges[1:2].astype(last_ref.dtype)


def stencil_call(step, emit, q, *extra):
    count, levels, rows, cols = q.shape
    planes = levels * rows
    outs = []
    if step:
        outs.append(jax.ShapeDtypeStruct(q.shape, q.dtype))
    if emit:
        outs += [
            jax.ShapeDtypeStruct((count, levels, cols), q.dtype),
            jax.ShapeDtypeStruct((count, levels, cols), q.dtype),
            jax.ShapeDtypeStruct((1, count * planes), q.dtype),
            jax.ShapeDtypeStruct((1, count * planes), q.dtype),
        ]
    vmem = pl.BlockSpec(memory_space=pltpu.VMEM)
    return pl.pallas_call(
        functools.partial(stencil_kernel, step, emit),
        out_shape=tuple(outs),
        in_specs=[vmem] * (1 + len(extra)),
        out_specs=tuple([vmem] * len(outs)),
        scratch_shapes=[
            pltpu.VMEM((levels, rows, cols), jnp.float32),
            pltpu.VMEM((LEVEL_BLOCK, rows, cols), jnp.float32),
            pltpu.VMEM((2, count, levels, cols), jnp.float32),
            pltpu.VMEM((count * planes, cols), jnp.float32),
            pltpu.VMEM((4, levels, rows, cols), jnp.float32),
        ],
    )(q, *extra)


def exchange(top, bottom, first, last):
    sec = lax.axis_size("sec")
    tile = lax.axis_size("tile")
    north = lax.ppermute(top, "sec", [(i, (i - 1) % sec) for i in range(sec)])
    south = lax.ppermute(bottom, "sec", [(i, (i + 1) % sec) for i in range(sec)])
    east = lax.ppermute(first, "tile", [(i, (i - 1) % tile) for i in range(tile)])
    west = lax.ppermute(last, "tile", [(i, (i + 1) % tile) for i in range(tile)])
    return north, south, east, west


def per_device(tracers, courant, destination, diffusion, band, band_table):
    count = tracers.shape[0]
    split = count // 2 if count % 2 == 0 and tracers.shape[2] <= 8 else count
    groups = [tracers[start:start + split] for start in range(0, count, split)]
    halos = [stencil_call(0, True, group) for group in groups]
    for step in range(STEPS):
        emit = step < STEPS - 1
        results = [
            stencil_call(1, emit, group, courant, *exchange(*halo))
            for group, halo in zip(groups, halos)
        ]
        groups = [result[0] for result in results]
        halos = [result[1:] for result in results]
    advected = jnp.concatenate(groups, axis=0) if len(groups) > 1 else groups[0]
    order = jnp.argsort(destination[0])
    band_count = band_table.shape[0]
    ordered = jnp.take(advected, order, axis=2, mode="clip")
    received = lax.all_to_all(ordered, "tile", split_axis=2, concat_axis=2, tiled=True)
    inverse = diffusion[0]
    diffused = jnp.einsum("kl,tlxy->tkxy", inverse, received, preferred_element_type=jnp.float32)
    diffused16 = diffused.astype(jnp.bfloat16)
    picked = (jnp.arange(band_count, dtype=jnp.int32) == band[0])[:, None, None]
    radiation = jnp.sum(jnp.where(picked, band_table, jnp.zeros_like(band_table)), axis=0)
    heating = jnp.einsum("kl,tlxy->tkxy", radiation, diffused16, preferred_element_type=jnp.float32)
    return (diffused + heating).astype(jnp.bfloat16)


def solution(mesh):
    placed = (
        P(None, None, "sec", "tile"),
        P(None, None, "sec", "tile"),
        P(("sec", "tile"), None),
        P(("sec", "tile"), None, None),
        P(("sec", "tile")),
        P(),
    )
    return jax.shard_map(
        per_device,
        mesh=mesh,
        in_specs=placed,
        out_specs=P(None, None, ("sec", "tile"), None),
        check_vma=False,
    )
```

```python
import functools

import jax
import jax.numpy as jnp
from jax import lax
from jax.experimental import pallas as pl
from jax.experimental.pallas import tpu as pltpu
from jax.sharding import PartitionSpec as P

STEPS = 3


LEVEL_BLOCK = 8


def stencil_kernel(step, emit, *refs):
    if step:
        q_ref, wind_ref, north_ref, south_ref, east_ref, west_ref = refs[:6]
        refs = refs[6:]
    else:
        q_ref = refs[0]
        refs = refs[1:]
    if step:
        out_ref = refs[0]
        refs = refs[1:]
    if emit:
        top_ref, bottom_ref, first_ref, last_ref = refs[:4]
        refs = refs[4:]
    new_scr, row_scr, halo_scr, side_scr, factor_scr = refs

    count, levels, rows, cols = q_ref.shape
    planes = levels * rows
    block = LEVEL_BLOCK if levels % LEVEL_BLOCK == 0 else 1

    if step:
        strips = jnp.zeros((cols, count * planes), jnp.float32)
        strips = jnp.where(
            lax.broadcasted_iota(jnp.int32, strips.shape, 0) == 0,
            east_ref[...].astype(jnp.float32),
            jnp.where(
                lax.broadcasted_iota(jnp.int32, strips.shape, 0) == 1,
                west_ref[...].astype(jnp.float32),
                strips,
            ),
        )
        side_scr[...] = strips.T
        halo_scr[0] = north_ref[...].astype(jnp.float32)
        halo_scr[1] = south_ref[...].astype(jnp.float32)
        sub = lax.broadcasted_iota(jnp.int32, (block, rows, cols), 1)
        lane = lax.broadcasted_iota(jnp.int32, (block, rows, cols), 2)
        for index in range(levels // block):
            levels_here = pl.ds(index * block, block)
            cx = wind_ref[0, levels_here].astype(jnp.float32)
            cy = wind_ref[1, levels_here].astype(jnp.float32)
            half_x = 0.5 * cx
            half_y = 0.5 * cy
            factor_scr[0, levels_here] = half_x
            factor_scr[1, levels_here] = half_x * cx
            factor_scr[2, levels_here] = half_y
            factor_scr[3, levels_here] = half_y * cy

    for field in range(count):
        if step:
            for index in range(levels // block):
                first = index * block
                levels_here = pl.ds(first, block)
                centre = q_ref[field, levels_here].astype(jnp.float32)
                half_x = factor_scr[0, levels_here]
                full_x = factor_scr[1, levels_here]
                half_y = factor_scr[2, levels_here]
                full_y = factor_scr[3, levels_here]
                row_scr[:, rows - 1, :] = halo_scr[0, field, levels_here]
                north = jnp.where(sub == rows - 1, row_scr[...], pltpu.roll(centre, rows - 1, 1))
                row_scr[:, 0, :] = halo_scr[1, field, levels_here]
                south = jnp.where(sub == 0, row_scr[...], pltpu.roll(centre, 1, 1))
                offset = field * planes + first * rows
                side = side_scr[pl.ds(offset, block * rows)].reshape(block, rows, cols)
                side = pltpu.roll(side, cols - 1, 2)
                east = jnp.where(lane == cols - 1, side, pltpu.roll(centre, cols - 1, 2))
                west = jnp.where(lane == 0, side, pltpu.roll(centre, 1, 2))
                out = centre - half_x * (north - south) + full_x * (north - 2.0 * centre + south)
                out = out - half_y * (east - west) + full_y * (east - 2.0 * centre + west)
                new = out.astype(jnp.bfloat16)
                out_ref[field, levels_here] = new
                if emit:
                    new_scr[levels_here] = new.astype(jnp.float32)
        elif emit:
            new_scr[...] = q_ref[field].astype(jnp.float32)
        if emit:
            top_ref[field] = new_scr[:, 0, :].astype(top_ref.dtype)
            bottom_ref[field] = new_scr[:, rows - 1, :].astype(bottom_ref.dtype)
            flat = new_scr[...].reshape(planes, cols).astype(jnp.bfloat16)
            pick = lax.broadcasted_iota(jnp.int32, (8, cols), 1)
            which = lax.broadcasted_iota(jnp.int32, (8, cols), 0)
            onehot = jnp.where(
                ((which == 0) & (pick == 0)) | ((which == 1) & (pick == cols - 1)), 1.0, 0.0
            ).astype(jnp.bfloat16)
            edges = lax.dot_general(
                onehot, flat, (((1,), (1,)), ((), ())), preferred_element_type=jnp.float32
            )
            first_ref[:, field * planes:(field + 1) * planes] = edges[0:1].astype(first_ref.dtype)
            last_ref[:, field * planes:(field + 1) * planes] = edges[1:2].astype(last_ref.dtype)


def stencil_call(step, emit, q, *extra):
    count, levels, rows, cols = q.shape
    planes = levels * rows
    outs = []
    if step:
        outs.append(jax.ShapeDtypeStruct(q.shape, q.dtype))
    if emit:
        outs += [
            jax.ShapeDtypeStruct((count, levels, cols), q.dtype),
            jax.ShapeDtypeStruct((count, levels, cols), q.dtype),
            jax.ShapeDtypeStruct((1, count * planes), q.dtype),
            jax.ShapeDtypeStruct((1, count * planes), q.dtype),
        ]
    vmem = pl.BlockSpec(memory_space=pltpu.VMEM)
    return pl.pallas_call(
        functools.partial(stencil_kernel, step, emit),
        out_shape=tuple(outs),
        in_specs=[vmem] * (1 + len(extra)),
        out_specs=tuple([vmem] * len(outs)),
        scratch_shapes=[
            pltpu.VMEM((levels, rows, cols), jnp.float32),
            pltpu.VMEM((LEVEL_BLOCK, rows, cols), jnp.float32),
            pltpu.VMEM((2, count, levels, cols), jnp.float32),
            pltpu.VMEM((count * planes, cols), jnp.float32),
            pltpu.VMEM((4, levels, rows, cols), jnp.float32),
        ],
    )(q, *extra)


def exchange(top, bottom, first, last):
    sec = lax.axis_size("sec")
    tile = lax.axis_size("tile")
    north = lax.ppermute(top, "sec", [(i, (i - 1) % sec) for i in range(sec)])
    south = lax.ppermute(bottom, "sec", [(i, (i + 1) % sec) for i in range(sec)])
    east = lax.ppermute(first, "tile", [(i, (i - 1) % tile) for i in range(tile)])
    west = lax.ppermute(last, "tile", [(i, (i + 1) % tile) for i in range(tile)])
    return north, south, east, west


def per_device(tracers, courant, destination, diffusion, band, band_table):
    halos = stencil_call(0, True, tracers)
    advected = tracers
    for step in range(STEPS):
        emit = step < STEPS - 1
        result = stencil_call(1, emit, advected, courant, *exchange(*halos))
        advected = result[0]
        halos = result[1:]
    order = jnp.argsort(destination[0])
    band_count = band_table.shape[0]
    rows = advected.shape[2]
    pick = (order[:, None] == jnp.arange(rows, dtype=order.dtype)[None, :]).astype(advected.dtype)
    ordered = jnp.einsum(
        "jg,flgy->fljy", pick, advected, preferred_element_type=jnp.float32
    ).astype(advected.dtype)
    received = lax.all_to_all(ordered, "tile", split_axis=2, concat_axis=2, tiled=True)
    inverse = diffusion[0]
    diffused = jnp.einsum("kl,tlxy->tkxy", inverse, received, preferred_element_type=jnp.float32)
    diffused16 = diffused.astype(jnp.bfloat16)
    picked = (jnp.arange(band_count, dtype=jnp.int32) == band[0])[:, None, None]
    radiation = jnp.sum(jnp.where(picked, band_table, jnp.zeros_like(band_table)), axis=0)
    heating = jnp.einsum("kl,tlxy->tkxy", radiation, diffused16, preferred_element_type=jnp.float32)
    return (diffused + heating).astype(jnp.bfloat16)


def solution(mesh):
    placed = (
        P(None, None, "sec", "tile"),
        P(None, None, "sec", "tile"),
        P(("sec", "tile"), None),
        P(("sec", "tile"), None, None),
        P(("sec", "tile")),
        P(),
    )
    return jax.shard_map(
        per_device,
        mesh=mesh,
        in_specs=placed,
        out_specs=P(None, None, ("sec", "tile"), None),
        check_vma=False,
    )
```

```python
import functools

import jax
import jax.numpy as jnp
from jax import lax
from jax.experimental import pallas as pl
from jax.experimental.pallas import tpu as pltpu
from jax.sharding import PartitionSpec as P

STEPS = 3


LEVEL_BLOCK = 4


def stencil_kernel(step, emit, *refs):
    if step:
        q_ref, wind_ref, north_ref, south_ref, east_ref, west_ref = refs[:6]
        refs = refs[6:]
    else:
        q_ref = refs[0]
        refs = refs[1:]
    if step:
        out_ref = refs[0]
        refs = refs[1:]
    if emit:
        top_ref, bottom_ref, first_ref, last_ref = refs[:4]
        refs = refs[4:]
    new_scr, row_scr, halo_scr, side_scr, factor_scr = refs

    count, levels, rows, cols = q_ref.shape
    planes = levels * rows
    block = LEVEL_BLOCK if levels % LEVEL_BLOCK == 0 else 1

    if step:
        strips = jnp.zeros((cols, count * planes), jnp.float32)
        strips = jnp.where(
            lax.broadcasted_iota(jnp.int32, strips.shape, 0) == 0,
            east_ref[...].astype(jnp.float32),
            jnp.where(
                lax.broadcasted_iota(jnp.int32, strips.shape, 0) == 1,
                west_ref[...].astype(jnp.float32),
                strips,
            ),
        )
        side_scr[...] = strips.T
        halo_scr[0] = north_ref[...].astype(jnp.float32)
        halo_scr[1] = south_ref[...].astype(jnp.float32)
        sub = lax.broadcasted_iota(jnp.int32, (block, rows, cols), 1)
        lane = lax.broadcasted_iota(jnp.int32, (block, rows, cols), 2)
        for index in range(levels // block):
            levels_here = pl.ds(index * block, block)
            cx = wind_ref[0, levels_here].astype(jnp.float32)
            cy = wind_ref[1, levels_here].astype(jnp.float32)
            half_x = 0.5 * cx
            half_y = 0.5 * cy
            factor_scr[0, levels_here] = half_x
            factor_scr[1, levels_here] = half_x * cx
            factor_scr[2, levels_here] = half_y
            factor_scr[3, levels_here] = half_y * cy

    for field in range(count):
        if step:
            for index in range(levels // block):
                first = index * block
                levels_here = pl.ds(first, block)
                centre = q_ref[field, levels_here].astype(jnp.float32)
                half_x = factor_scr[0, levels_here]
                full_x = factor_scr[1, levels_here]
                half_y = factor_scr[2, levels_here]
                full_y = factor_scr[3, levels_here]
                row_scr[:, rows - 1, :] = halo_scr[0, field, levels_here]
                north = jnp.where(sub == rows - 1, row_scr[...], pltpu.roll(centre, rows - 1, 1))
                row_scr[:, 0, :] = halo_scr[1, field, levels_here]
                south = jnp.where(sub == 0, row_scr[...], pltpu.roll(centre, 1, 1))
                offset = field * planes + first * rows
                side = side_scr[pl.ds(offset, block * rows)].reshape(block, rows, cols)
                side = pltpu.roll(side, cols - 1, 2)
                east = jnp.where(lane == cols - 1, side, pltpu.roll(centre, cols - 1, 2))
                west = jnp.where(lane == 0, side, pltpu.roll(centre, 1, 2))
                out = centre - half_x * (north - south) + full_x * (north - 2.0 * centre + south)
                out = out - half_y * (east - west) + full_y * (east - 2.0 * centre + west)
                new = out.astype(jnp.bfloat16)
                out_ref[field, levels_here] = new
                if emit:
                    new_scr[levels_here] = new.astype(jnp.float32)
        elif emit:
            new_scr[...] = q_ref[field].astype(jnp.float32)
        if emit:
            top_ref[field] = new_scr[:, 0, :].astype(top_ref.dtype)
            bottom_ref[field] = new_scr[:, rows - 1, :].astype(bottom_ref.dtype)
            flat = new_scr[...].reshape(planes, cols).astype(jnp.bfloat16)
            pick = lax.broadcasted_iota(jnp.int32, (8, cols), 1)
            which = lax.broadcasted_iota(jnp.int32, (8, cols), 0)
            onehot = jnp.where(
                ((which == 0) & (pick == 0)) | ((which == 1) & (pick == cols - 1)), 1.0, 0.0
            ).astype(jnp.bfloat16)
            edges = lax.dot_general(
                onehot, flat, (((1,), (1,)), ((), ())), preferred_element_type=jnp.float32
            )
            first_ref[:, field * planes:(field + 1) * planes] = edges[0:1].astype(first_ref.dtype)
            last_ref[:, field * planes:(field + 1) * planes] = edges[1:2].astype(last_ref.dtype)


def stencil_call(step, emit, q, *extra):
    count, levels, rows, cols = q.shape
    planes = levels * rows
    outs = []
    if step:
        outs.append(jax.ShapeDtypeStruct(q.shape, q.dtype))
    if emit:
        outs += [
            jax.ShapeDtypeStruct((count, levels, cols), q.dtype),
            jax.ShapeDtypeStruct((count, levels, cols), q.dtype),
            jax.ShapeDtypeStruct((1, count * planes), q.dtype),
            jax.ShapeDtypeStruct((1, count * planes), q.dtype),
        ]
    vmem = pl.BlockSpec(memory_space=pltpu.VMEM)
    return pl.pallas_call(
        functools.partial(stencil_kernel, step, emit),
        out_shape=tuple(outs),
        in_specs=[vmem] * (1 + len(extra)),
        out_specs=tuple([vmem] * len(outs)),
        scratch_shapes=[
            pltpu.VMEM((levels, rows, cols), jnp.float32),
            pltpu.VMEM((LEVEL_BLOCK, rows, cols), jnp.float32),
            pltpu.VMEM((2, count, levels, cols), jnp.float32),
            pltpu.VMEM((count * planes, cols), jnp.float32),
            pltpu.VMEM((4, levels, rows, cols), jnp.float32),
        ],
    )(q, *extra)


def exchange(top, bottom, first, last):
    sec = lax.axis_size("sec")
    tile = lax.axis_size("tile")
    north = lax.ppermute(top, "sec", [(i, (i - 1) % sec) for i in range(sec)])
    south = lax.ppermute(bottom, "sec", [(i, (i + 1) % sec) for i in range(sec)])
    east = lax.ppermute(first, "tile", [(i, (i - 1) % tile) for i in range(tile)])
    west = lax.ppermute(last, "tile", [(i, (i + 1) % tile) for i in range(tile)])
    return north, south, east, west


def per_device(tracers, courant, destination, diffusion, band, band_table):
    halos = stencil_call(0, True, tracers)
    advected = tracers
    for step in range(STEPS):
        emit = step < STEPS - 1
        result = stencil_call(1, emit, advected, courant, *exchange(*halos))
        advected = result[0]
        halos = result[1:]
    order = jnp.argsort(destination[0])
    band_count = band_table.shape[0]
    rows = advected.shape[2]
    pick = (order[:, None] == jnp.arange(rows, dtype=order.dtype)[None, :]).astype(advected.dtype)
    ordered = jnp.einsum(
        "jg,flgy->fljy", pick, advected, preferred_element_type=jnp.float32
    ).astype(advected.dtype)
    received = lax.all_to_all(ordered, "tile", split_axis=2, concat_axis=2, tiled=True)
    inverse = diffusion[0]
    diffused = jnp.einsum("kl,tlxy->tkxy", inverse, received, preferred_element_type=jnp.float32)
    diffused16 = diffused.astype(jnp.bfloat16)
    picked = (jnp.arange(band_count, dtype=jnp.int32) == band[0])[:, None, None]
    radiation = jnp.sum(jnp.where(picked, band_table, jnp.zeros_like(band_table)), axis=0)
    heating = jnp.einsum("kl,tlxy->tkxy", radiation, diffused16, preferred_element_type=jnp.float32)
    return (diffused + heating).astype(jnp.bfloat16)


def solution(mesh):
    placed = (
        P(None, None, "sec", "tile"),
        P(None, None, "sec", "tile"),
        P(("sec", "tile"), None),
        P(("sec", "tile"), None, None),
        P(("sec", "tile")),
        P(),
    )
    return jax.shard_map(
        per_device,
        mesh=mesh,
        in_specs=placed,
        out_specs=P(None, None, ("sec", "tile"), None),
        check_vma=False,
    )
```

```python
import functools

import jax
import jax.numpy as jnp
from jax import lax
from jax.experimental import pallas as pl
from jax.experimental.pallas import tpu as pltpu
from jax.sharding import PartitionSpec as P

STEPS = 3


LEVEL_BLOCK = 4


def stencil_kernel(step, emit, *refs):
    if step:
        q_ref, wind_ref, north_ref, south_ref, east_ref, west_ref = refs[:6]
        refs = refs[6:]
    else:
        q_ref = refs[0]
        refs = refs[1:]
    if step:
        out_ref = refs[0]
        refs = refs[1:]
    if emit:
        top_ref, bottom_ref, first_ref, last_ref = refs[:4]
        refs = refs[4:]
    new_scr, row_scr, halo_scr, side_scr, factor_scr = refs

    count, levels, rows, cols = q_ref.shape
    planes = levels * rows
    block = LEVEL_BLOCK if levels % LEVEL_BLOCK == 0 else 1

    if step:
        strips = jnp.zeros((cols, count * planes), jnp.float32)
        strips = jnp.where(
            lax.broadcasted_iota(jnp.int32, strips.shape, 0) == 0,
            east_ref[...].astype(jnp.float32),
            jnp.where(
                lax.broadcasted_iota(jnp.int32, strips.shape, 0) == 1,
                west_ref[...].astype(jnp.float32),
                strips,
            ),
        )
        side_scr[...] = strips.T
        halo_scr[0] = north_ref[...].astype(jnp.float32)
        halo_scr[1] = south_ref[...].astype(jnp.float32)
        sub = lax.broadcasted_iota(jnp.int32, (block, rows, cols), 1)
        lane = lax.broadcasted_iota(jnp.int32, (block, rows, cols), 2)
        for index in range(levels // block):
            levels_here = pl.ds(index * block, block)
            cx = wind_ref[0, levels_here].astype(jnp.float32)
            cy = wind_ref[1, levels_here].astype(jnp.float32)
            half_x = 0.5 * cx
            half_y = 0.5 * cy
            factor_scr[0, levels_here] = half_x
            factor_scr[1, levels_here] = half_x * cx
            factor_scr[2, levels_here] = half_y
            factor_scr[3, levels_here] = half_y * cy

    for field in range(count):
        if step:
            for index in range(levels // block):
                first = index * block
                levels_here = pl.ds(first, block)
                centre = q_ref[field, levels_here].astype(jnp.float32)
                half_x = factor_scr[0, levels_here]
                full_x = factor_scr[1, levels_here]
                half_y = factor_scr[2, levels_here]
                full_y = factor_scr[3, levels_here]
                row_scr[:, rows - 1, :] = halo_scr[0, field, levels_here]
                north = jnp.where(sub == rows - 1, row_scr[...], pltpu.roll(centre, rows - 1, 1))
                row_scr[:, 0, :] = halo_scr[1, field, levels_here]
                south = jnp.where(sub == 0, row_scr[...], pltpu.roll(centre, 1, 1))
                offset = field * planes + first * rows
                side = side_scr[pl.ds(offset, block * rows)].reshape(block, rows, cols)
                side = pltpu.roll(side, cols - 1, 2)
                east = jnp.where(lane == cols - 1, side, pltpu.roll(centre, cols - 1, 2))
                west = jnp.where(lane == 0, side, pltpu.roll(centre, 1, 2))
                out = centre - half_x * (north - south) + full_x * (north - 2.0 * centre + south)
                out = out - half_y * (east - west) + full_y * (east - 2.0 * centre + west)
                new = out.astype(jnp.bfloat16)
                out_ref[field, levels_here] = new
                if emit:
                    widened = new.astype(jnp.float32)
                    new_scr[levels_here] = widened
                    top_ref[field, levels_here] = widened[:, 0, :].astype(top_ref.dtype)
                    bottom_ref[field, levels_here] = widened[:, rows - 1, :].astype(bottom_ref.dtype)
        elif emit:
            new_scr[...] = q_ref[field].astype(jnp.float32)
        if emit and not step:
            top_ref[field] = new_scr[:, 0, :].astype(top_ref.dtype)
            bottom_ref[field] = new_scr[:, rows - 1, :].astype(bottom_ref.dtype)
        if emit:
            flat = new_scr[...].reshape(planes, cols).astype(jnp.bfloat16)
            pick = lax.broadcasted_iota(jnp.int32, (8, cols), 1)
            which = lax.broadcasted_iota(jnp.int32, (8, cols), 0)
            onehot = jnp.where(
                ((which == 0) & (pick == 0)) | ((which == 1) & (pick == cols - 1)), 1.0, 0.0
            ).astype(jnp.bfloat16)
            edges = lax.dot_general(
                onehot, flat, (((1,), (1,)), ((), ())), preferred_element_type=jnp.float32
            )
            first_ref[:, field * planes:(field + 1) * planes] = edges[0:1].astype(first_ref.dtype)
            last_ref[:, field * planes:(field + 1) * planes] = edges[1:2].astype(last_ref.dtype)


def stencil_call(step, emit, q, *extra):
    count, levels, rows, cols = q.shape
    planes = levels * rows
    outs = []
    if step:
        outs.append(jax.ShapeDtypeStruct(q.shape, q.dtype))
    if emit:
        outs += [
            jax.ShapeDtypeStruct((count, levels, cols), q.dtype),
            jax.ShapeDtypeStruct((count, levels, cols), q.dtype),
            jax.ShapeDtypeStruct((1, count * planes), q.dtype),
            jax.ShapeDtypeStruct((1, count * planes), q.dtype),
        ]
    vmem = pl.BlockSpec(memory_space=pltpu.VMEM)
    return pl.pallas_call(
        functools.partial(stencil_kernel, step, emit),
        out_shape=tuple(outs),
        in_specs=[vmem] * (1 + len(extra)),
        out_specs=tuple([vmem] * len(outs)),
        scratch_shapes=[
            pltpu.VMEM((levels, rows, cols), jnp.float32),
            pltpu.VMEM((LEVEL_BLOCK, rows, cols), jnp.float32),
            pltpu.VMEM((2, count, levels, cols), jnp.float32),
            pltpu.VMEM((count * planes, cols), jnp.float32),
            pltpu.VMEM((4, levels, rows, cols), jnp.float32),
        ],
    )(q, *extra)


def exchange(top, bottom, first, last):
    sec = lax.axis_size("sec")
    tile = lax.axis_size("tile")
    north = lax.ppermute(top, "sec", [(i, (i - 1) % sec) for i in range(sec)])
    south = lax.ppermute(bottom, "sec", [(i, (i + 1) % sec) for i in range(sec)])
    east = lax.ppermute(first, "tile", [(i, (i - 1) % tile) for i in range(tile)])
    west = lax.ppermute(last, "tile", [(i, (i + 1) % tile) for i in range(tile)])
    return north, south, east, west


def per_device(tracers, courant, destination, diffusion, band, band_table):
    halos = stencil_call(0, True, tracers)
    advected = tracers
    for step in range(STEPS):
        emit = step < STEPS - 1
        result = stencil_call(1, emit, advected, courant, *exchange(*halos))
        advected = result[0]
        halos = result[1:]
    order = jnp.argsort(destination[0])
    band_count = band_table.shape[0]
    rows = advected.shape[2]
    pick = (order[:, None] == jnp.arange(rows, dtype=order.dtype)[None, :]).astype(advected.dtype)
    ordered = jnp.einsum(
        "jg,flgy->fljy", pick, advected, preferred_element_type=jnp.float32
    ).astype(advected.dtype)
    received = lax.all_to_all(ordered, "tile", split_axis=2, concat_axis=2, tiled=True)
    inverse = diffusion[0]
    diffused = jnp.einsum("kl,tlxy->tkxy", inverse, received, preferred_element_type=jnp.float32)
    diffused16 = diffused.astype(jnp.bfloat16)
    picked = (jnp.arange(band_count, dtype=jnp.int32) == band[0])[:, None, None]
    radiation = jnp.sum(jnp.where(picked, band_table, jnp.zeros_like(band_table)), axis=0)
    heating = jnp.einsum("kl,tlxy->tkxy", radiation, diffused16, preferred_element_type=jnp.float32)
    return (diffused + heating).astype(jnp.bfloat16)


def solution(mesh):
    placed = (
        P(None, None, "sec", "tile"),
        P(None, None, "sec", "tile"),
        P(("sec", "tile"), None),
        P(("sec", "tile"), None, None),
        P(("sec", "tile")),
        P(),
    )
    return jax.shard_map(
        per_device,
        mesh=mesh,
        in_specs=placed,
        out_specs=P(None, None, ("sec", "tile"), None),
        check_vma=False,
    )
```

```python
import functools

import jax
import jax.numpy as jnp
from jax import lax
from jax.experimental import pallas as pl
from jax.experimental.pallas import tpu as pltpu
from jax.sharding import PartitionSpec as P

STEPS = 3


LEVEL_BLOCK = 4


def stencil_kernel(step, emit, *refs):
    if step:
        q_ref, wind_ref, north_ref, south_ref, east_ref, west_ref = refs[:6]
        refs = refs[6:]
    else:
        q_ref = refs[0]
        refs = refs[1:]
    if step:
        out_ref = refs[0]
        refs = refs[1:]
    if emit:
        top_ref, bottom_ref, first_ref, last_ref = refs[:4]
        refs = refs[4:]
    new_scr, row_scr, halo_scr, side_scr, factor_scr = refs

    count, levels, rows, cols = q_ref.shape
    planes = levels * rows
    block = LEVEL_BLOCK if levels % LEVEL_BLOCK == 0 else 1

    if step:
        strips = jnp.zeros((cols, count * planes), jnp.float32)
        strips = jnp.where(
            lax.broadcasted_iota(jnp.int32, strips.shape, 0) == 0,
            east_ref[...].astype(jnp.float32),
            jnp.where(
                lax.broadcasted_iota(jnp.int32, strips.shape, 0) == 1,
                west_ref[...].astype(jnp.float32),
                strips,
            ),
        )
        side_scr[...] = strips.T
        halo_scr[0] = north_ref[...].astype(jnp.float32)
        halo_scr[1] = south_ref[...].astype(jnp.float32)
        sub = lax.broadcasted_iota(jnp.int32, (block, rows, cols), 1)
        lane = lax.broadcasted_iota(jnp.int32, (block, rows, cols), 2)
        for index in range(levels // block):
            levels_here = pl.ds(index * block, block)
            cx = wind_ref[0, levels_here].astype(jnp.float32)
            cy = wind_ref[1, levels_here].astype(jnp.float32)
            half_x = 0.5 * cx
            half_y = 0.5 * cy
            factor_scr[0, levels_here] = half_x
            factor_scr[1, levels_here] = half_x * cx
            factor_scr[2, levels_here] = half_y
            factor_scr[3, levels_here] = half_y * cy

    for field in range(count):
        if step:
            for index in range(levels // block):
                first = index * block
                levels_here = pl.ds(first, block)
                centre = q_ref[field, levels_here].astype(jnp.float32)
                half_x = factor_scr[0, levels_here]
                full_x = factor_scr[1, levels_here]
                half_y = factor_scr[2, levels_here]
                full_y = factor_scr[3, levels_here]
                row_scr[:, rows - 1, :] = halo_scr[0, field, levels_here]
                north = jnp.where(sub == rows - 1, row_scr[...], pltpu.roll(centre, rows - 1, 1))
                row_scr[:, 0, :] = halo_scr[1, field, levels_here]
                south = jnp.where(sub == 0, row_scr[...], pltpu.roll(centre, 1, 1))
                offset = field * planes + first * rows
                side = side_scr[pl.ds(offset, block * rows)].reshape(block, rows, cols)
                side = pltpu.roll(side, cols - 1, 2)
                east = jnp.where(lane == cols - 1, side, pltpu.roll(centre, cols - 1, 2))
                west = jnp.where(lane == 0, side, pltpu.roll(centre, 1, 2))
                out = centre - half_x * (north - south) + full_x * (north - 2.0 * centre + south)
                out = out - half_y * (east - west) + full_y * (east - 2.0 * centre + west)
                new = out.astype(jnp.bfloat16)
                out_ref[field, levels_here] = new
                if emit:
                    widened = new.astype(jnp.float32)
                    new_scr[levels_here] = widened
                    top_ref[field, levels_here] = widened[:, 0, :].astype(top_ref.dtype)
                    bottom_ref[field, levels_here] = widened[:, rows - 1, :].astype(bottom_ref.dtype)
        elif emit:
            for index in range(levels // block):
                levels_here = pl.ds(index * block, block)
                widened = q_ref[field, levels_here].astype(jnp.float32)
                new_scr[levels_here] = widened
                top_ref[field, levels_here] = widened[:, 0, :].astype(top_ref.dtype)
                bottom_ref[field, levels_here] = widened[:, rows - 1, :].astype(bottom_ref.dtype)
        if emit:
            flat = new_scr[...].reshape(planes, cols).astype(jnp.bfloat16)
            pick = lax.broadcasted_iota(jnp.int32, (8, cols), 1)
            which = lax.broadcasted_iota(jnp.int32, (8, cols), 0)
            onehot = jnp.where(
                ((which == 0) & (pick == 0)) | ((which == 1) & (pick == cols - 1)), 1.0, 0.0
            ).astype(jnp.bfloat16)
            edges = lax.dot_general(
                onehot, flat, (((1,), (1,)), ((), ())), preferred_element_type=jnp.float32
            )
            first_ref[:, field * planes:(field + 1) * planes] = edges[0:1].astype(first_ref.dtype)
            last_ref[:, field * planes:(field + 1) * planes] = edges[1:2].astype(last_ref.dtype)


def stencil_call(step, emit, q, *extra):
    count, levels, rows, cols = q.shape
    planes = levels * rows
    outs = []
    if step:
        outs.append(jax.ShapeDtypeStruct(q.shape, q.dtype))
    if emit:
        outs += [
            jax.ShapeDtypeStruct((count, levels, cols), q.dtype),
            jax.ShapeDtypeStruct((count, levels, cols), q.dtype),
            jax.ShapeDtypeStruct((1, count * planes), q.dtype),
            jax.ShapeDtypeStruct((1, count * planes), q.dtype),
        ]
    vmem = pl.BlockSpec(memory_space=pltpu.VMEM)
    return pl.pallas_call(
        functools.partial(stencil_kernel, step, emit),
        out_shape=tuple(outs),
        in_specs=[vmem] * (1 + len(extra)),
        out_specs=tuple([vmem] * len(outs)),
        scratch_shapes=[
            pltpu.VMEM((levels, rows, cols), jnp.float32),
            pltpu.VMEM((LEVEL_BLOCK, rows, cols), jnp.float32),
            pltpu.VMEM((2, count, levels, cols), jnp.float32),
            pltpu.VMEM((count * planes, cols), jnp.float32),
            pltpu.VMEM((4, levels, rows, cols), jnp.float32),
        ],
    )(q, *extra)


def exchange(top, bottom, first, last):
    sec = lax.axis_size("sec")
    tile = lax.axis_size("tile")
    north = lax.ppermute(top, "sec", [(i, (i - 1) % sec) for i in range(sec)])
    south = lax.ppermute(bottom, "sec", [(i, (i + 1) % sec) for i in range(sec)])
    east = lax.ppermute(first, "tile", [(i, (i - 1) % tile) for i in range(tile)])
    west = lax.ppermute(last, "tile", [(i, (i + 1) % tile) for i in range(tile)])
    return north, south, east, west


def per_device(tracers, courant, destination, diffusion, band, band_table):
    halos = stencil_call(0, True, tracers)
    advected = tracers
    for step in range(STEPS):
        emit = step < STEPS - 1
        result = stencil_call(1, emit, advected, courant, *exchange(*halos))
        advected = result[0]
        halos = result[1:]
    order = jnp.argsort(destination[0])
    band_count = band_table.shape[0]
    rows = advected.shape[2]
    pick = (order[:, None] == jnp.arange(rows, dtype=order.dtype)[None, :]).astype(advected.dtype)
    ordered = jnp.einsum(
        "jg,flgy->fljy", pick, advected, preferred_element_type=jnp.float32
    ).astype(advected.dtype)
    received = lax.all_to_all(ordered, "tile", split_axis=2, concat_axis=2, tiled=True)
    inverse = diffusion[0]
    diffused = jnp.einsum("kl,tlxy->tkxy", inverse, received, preferred_element_type=jnp.float32)
    diffused16 = diffused.astype(jnp.bfloat16)
    picked = (jnp.arange(band_count, dtype=jnp.int32) == band[0])[:, None, None]
    radiation = jnp.sum(jnp.where(picked, band_table, jnp.zeros_like(band_table)), axis=0)
    heating = jnp.einsum("kl,tlxy->tkxy", radiation, diffused16, preferred_element_type=jnp.float32)
    return (diffused + heating).astype(jnp.bfloat16)


def solution(mesh):
    placed = (
        P(None, None, "sec", "tile"),
        P(None, None, "sec", "tile"),
        P(("sec", "tile"), None),
        P(("sec", "tile"), None, None),
        P(("sec", "tile")),
        P(),
    )
    return jax.shard_map(
        per_device,
        mesh=mesh,
        in_specs=placed,
        out_specs=P(None, None, ("sec", "tile"), None),
        check_vma=False,
    )
```
